32 devices in a mesh: prow: 4 (over y, x), pcol: 4 (over z), cuts: 2 (over core).
Axes of the slice: x: 2, y: 2, z: 4, core: 2. Of those that a mesh axis runs over, the one named last changes fastest.
Arguments:
- amplitudes: bfloat16 [6144, 6400], P('prow', 'cuts'), may hold values from -6 to 6
- integrals: bfloat16 [6400, 1600], P(('cuts', 'prow'), 'pcol'), may hold values from -0.21875 to 0.21875
- irrep_rows: int32 [6400], replicated, may hold values from 0 to 7, as said below
- irrep_cols: int32 [1600], P('pcol'), may hold values from 0 to 7, as said below
- mirror_row: int32 [6144], replicated, may hold values from 0 to 6143, as said below
Outputs:
- residual: float32 [6144, 1600], P(('prow', 'cuts'), 'pcol')
The draws below stay inside these ranges and needn't reach their ends.
Inputs may be any that keep to these rules, and one draw needn't show every extreme that they name: irrep_rows is non-decreasing along the contraction pairs (pairs sorted by irrep, tiles of uneven size), and every one of the 8 irreps holds at least one pair. Some aligned run of 800 pairs carries a single irrep, and that irrep also covers some whole aligned run of 400 columns, so the mask of that tile is all ones. irrep_cols is non-decreasing along the columns (tiles of uneven size), and every one of the 8 irreps holds at least one column. Some aligned run of 400 columns carries a single irrep. mirror_row is an involution without fixed points. Rows are grouped into 8 aligned blocks of 768 rows, block b = r * 2 + c; the partner of every row of block (r, c) lies in block (r XOR (2), c).
All inputs are finite; a program needn't handle non-finite values.
Results may differ from the reference program's by a relative error of at most 0.0003.
Values may be sent and summed in bfloat16 or wider, within the bound.
No kernel may reach another device: no remote copies, remote signals or barrier semaphores. Data moves between devices by JAX's collectives and lax.ppermute only.
A program may use at most 64 MiB of HBM per device.

```python
import jax
import jax.numpy as jnp

NIRREP = 8
PR_DEV = 1536
QC_DEV = 400
KDIM = 6400
PROWS = 6144
QCOLS = 1600
N_PROW = 4
N_CUTS = 2


def shared_irrep(key):
    return jax.random.randint(jax.random.fold_in(key, 0), (), 0, NIRREP).astype(jnp.int32)


def tile_labels(key, salt, total, big):
    chosen = shared_irrep(key)
    weights = jax.random.randint(jax.random.fold_in(key, salt), (NIRREP,), 1, 5).astype(jnp.int32)
    irreps = jnp.arange(NIRREP, dtype=jnp.int32)
    is_big = irreps == chosen
    others = jnp.where(is_big, 0, weights).astype(jnp.int32)
    spare = total - big - (NIRREP - 1)
    sizes = jnp.where(is_big, big, 1 + spare * others // jnp.sum(others)).astype(jnp.int32)
    leftover = total - jnp.sum(sizes)
    target = jnp.where(chosen == 0, 1, 0).astype(jnp.int32)
    sizes = sizes + jnp.where(irreps == target, leftover, 0).astype(jnp.int32)
    ends = jnp.cumsum(sizes).astype(jnp.int32)
    places = jnp.arange(total, dtype=jnp.int32)
    labels = jnp.sum((places[:, None] >= ends[None, :NIRREP - 1]).astype(jnp.int32), axis=1)
    return labels.astype(jnp.int32)


def draw_irrep_rows(key, part):
    piece = KDIM // (N_CUTS * N_PROW)
    big = max(KDIM // 4, 2 * piece)
    return tile_labels(key, 1, KDIM, big)


def draw_irrep_cols(key, part):
    big = max(QCOLS // 4, 2 * QC_DEV)
    return tile_labels(key, 2, QCOLS, big)


def draw_mirror_row(key, part):
    half = N_PROW // 2
    block = PR_DEV // N_CUTS
    keys = jax.random.split(key, half * N_CUTS)
    perms = jax.vmap(lambda k: jax.random.permutation(k, block))(keys)
    perms = perms.astype(jnp.int32).reshape(half, N_CUTS, block)
    inverse = jnp.argsort(perms, axis=-1).astype(jnp.int32)
    lows = jnp.arange(half, dtype=jnp.int32)[:, None, None]
    cutsidx = jnp.arange(N_CUTS, dtype=jnp.int32)[None, :, None]
    upper_base = ((lows + half) * N_CUTS + cutsidx) * block
    lower_base = (lows * N_CUTS + cutsidx) * block
    first = upper_base + perms
    second = lower_base + inverse
    return jnp.concatenate([first, second], axis=0).reshape(-1).astype(jnp.int32)


def shard_levels(key, shape, cuts, least, largest):
    factor_of = 1.0
    for position, blocks in cuts:
        steps = jax.random.uniform(jax.random.fold_in(jax.random.fold_in(key, 6), position), (blocks,), jnp.float32, least / len(cuts), largest / len(cuts))
        factor_of = factor_of * jnp.repeat(jnp.exp(steps), shape[position] // blocks).reshape((-1,) + (1,) * (len(shape) - 1 - position))
    return factor_of


def bell_draw(key, dims, spread, limit, cuts=(), held_as=jnp.bfloat16):
    array = jax.random.normal(key, dims, jnp.float32) * spread
    if len(cuts) > 0:
        array = shard_levels(key, dims, cuts, -0.22, 0.18) * array
    return jnp.clip(array, min=-limit, max=limit).astype(held_as)


def setup_inputs(seed: int = 0) -> dict:
    streams_of = jax.random.split(jax.random.key(seed), 6)
    return {
        "amplitudes": bell_draw(streams_of[0], (PROWS, KDIM), 1.0, 6.0, ((0, 4), (1, 2))),
        "integrals": bell_draw(streams_of[1], (KDIM, QCOLS), (KDIM // NIRREP) ** -0.5, 0.21875, ((0, 8), (1, 4))),
        "irrep_rows": draw_irrep_rows(jax.random.fold_in(streams_of[5], 71), 0),
        "irrep_cols": draw_irrep_cols(jax.random.fold_in(streams_of[5], 71), 0),
        "mirror_row": draw_mirror_row(jax.random.fold_in(streams_of[5], 71), 0),
    }


def reference(amplitudes, integrals, irrep_rows, irrep_cols, mirror_row):
    same = irrep_rows[:, None] == irrep_cols[None, :]
    blocked = jnp.where(same, integrals, jnp.zeros_like(integrals))
    cycle = jnp.dot(amplitudes, blocked, preferred_element_type=jnp.float32)
    partner = jnp.take(cycle, mirror_row.astype(jnp.int32), axis=0)
    return cycle - partner
```

```python
import jax
import jax.numpy as jnp
from jax import lax
from jax.sharding import PartitionSpec as P


def swap(value, axis, mask):
    return lax.ppermute(value, axis, [(i, i ^ mask) for i in range(lax.axis_size(axis))])


def gather_prow(own, prow_idx, prow_count):
    count = own.shape[0]
    blocks = {0: own}
    if prow_count == 4:
        blocks[1] = swap(own, "prow", 1)
        blocks[2] = swap(own, "prow", 2)
        blocks[3] = swap(blocks[2], "prow", 1)
    else:
        for s in range(1, prow_count):
            blocks[s] = swap(own, "prow", s)
    piece = jnp.zeros((prow_count * count,) + own.shape[1:], own.dtype)
    for s, block in blocks.items():
        piece = lax.dynamic_update_slice(piece, block, (jnp.bitwise_xor(prow_idx, s) * count, 0))
    return piece


def reduce_cuts(terms, cuts_idx, cuts_count):
    rows = terms.shape[0] // cuts_count
    total = lax.dynamic_slice_in_dim(terms, cuts_idx * rows, rows, axis=0)
    for s in range(1, cuts_count):
        part = lax.dynamic_slice_in_dim(terms, jnp.bitwise_xor(cuts_idx, s) * rows, rows, axis=0)
        total = total + swap(part, "cuts", s)
    return total


def shards(amplitudes, integrals, irrep_rows, irrep_cols, mirror_row):
    prow_count = lax.axis_size("prow")
    cuts_count = lax.axis_size("cuts")
    slice_width = amplitudes.shape[1]
    prow_idx = lax.axis_index("prow")
    cuts_idx = lax.axis_index("cuts")
    piece = gather_prow(integrals, prow_idx, prow_count)
    count = piece.shape[0]
    labels = lax.dynamic_slice(irrep_rows, (cuts_idx * slice_width,), (count,))
    same = labels[:, None] == irrep_cols[None, :]
    blocked = jnp.where(same, piece, jnp.zeros_like(piece))
    terms = jnp.dot(amplitudes, blocked, preferred_element_type=jnp.float32)
    cycle = reduce_cuts(terms, cuts_idx, cuts_count)
    block_rows = cycle.shape[0]
    half = prow_count // 2
    own_block = prow_idx * cuts_count + cuts_idx
    partner_block = jnp.bitwise_xor(prow_idx, half) * cuts_count + cuts_idx
    mine = lax.dynamic_slice(mirror_row, (own_block * block_rows,), (block_rows,))
    local = mine - partner_block * block_rows
    fetched = swap(cycle, "prow", half)
    return cycle - jnp.take(fetched, local, axis=0)


def solution(mesh):
    placed = (P("prow", "cuts"), P(("cuts", "prow"), "pcol"), P(), P("pcol"), P())
    return jax.shard_map(
        shards, mesh=mesh, in_specs=placed, out_specs=P(("prow", "cuts"), "pcol"), check_vma=False
    )
```

```python
import jax
import jax.numpy as jnp
from jax import lax
from jax.experimental import pallas as pl
from jax.experimental.pallas import tpu as pltpu
from jax.sharding import PartitionSpec as P


def swap(value, axis, mask):
    return lax.ppermute(value, axis, [(i, i ^ mask) for i in range(lax.axis_size(axis))])


def gather_prow(own, prow_idx, prow_count):
    count = own.shape[0]
    if prow_count == 4 and count % 32 == 0:
        half = count // 2
        from_x = swap(own, "prow", 1)
        from_y = swap(own, "prow", 2)
        diag_a = swap(from_y[:half], "prow", 1)
        diag_b = swap(from_x[half:], "prow", 2)
        base = jnp.bitwise_xor(prow_idx, 3) * count
        return [(own, prow_idx * count), (from_x, jnp.bitwise_xor(prow_idx, 1) * count),
                (from_y, jnp.bitwise_xor(prow_idx, 2) * count), (diag_a, base), (diag_b, base + half)]
    blocks = [(own, prow_idx * count)]
    for s in range(1, prow_count):
        blocks.append((swap(own, "prow", s), jnp.bitwise_xor(prow_idx, s) * count))
    return blocks


def contract(amplitudes, blocks):
    rows, width = amplitudes.shape
    cols = blocks[0][0].shape[1]
    n = len(blocks)
    counts = [b.shape[0] for b, _ in blocks]
    if any(c % 16 for c in counts):
        piece = jnp.zeros((width, cols), blocks[0][0].dtype)
        for b, o in blocks:
            piece = lax.dynamic_update_slice(piece, b, (o, 0))
        return jnp.dot(amplitudes, piece, preferred_element_type=jnp.float32)
    offsets = jnp.stack([o for _, o in blocks]).astype(jnp.int32)
    tm = rows // 4 if rows % 32 == 0 else rows

    def kernel(off_ref, a_ref, *refs):
        w_refs = refs[:n]
        o_ref, wbuf, sem = refs[n:]

        @pl.when(pl.program_id(0) == 0)
        def _():
            copies = [pltpu.make_async_copy(w_refs[s], wbuf.at[pl.ds(pl.multiple_of(off_ref[s], 16), counts[s])], sem.at[s])
                      for s in range(n)]
            for c in copies:
                c.start()
            for c in copies:
                c.wait()

        o_ref[...] = jnp.dot(a_ref[...], wbuf[...], preferred_element_type=jnp.float32)

    grid_spec = pltpu.PrefetchScalarGridSpec(
        num_scalar_prefetch=1,
        grid=(rows // tm,),
        in_specs=[pl.BlockSpec((tm, width), lambda i, o: (i, 0))] + [pl.BlockSpec(memory_space=pl.ANY)] * n,
        out_specs=pl.BlockSpec((tm, cols), lambda i, o: (i, 0)),
        scratch_shapes=[pltpu.VMEM((width, cols), blocks[0][0].dtype), pltpu.SemaphoreType.DMA((n,))],
    )
    return pl.pallas_call(
        kernel,
        grid_spec=grid_spec,
        out_shape=jax.ShapeDtypeStruct((rows, cols), jnp.float32),
        compiler_params=pltpu.CompilerParams(dimension_semantics=("arbitrary",)),
    )(offsets, amplitudes, *[b for b, _ in blocks])


def reduce_cuts(terms, cuts_idx, cuts_count):
    rows = terms.shape[0] // cuts_count
    total = lax.dynamic_slice_in_dim(terms, cuts_idx * rows, rows, axis=0)
    for s in range(1, cuts_count):
        part = lax.dynamic_slice_in_dim(terms, jnp.bitwise_xor(cuts_idx, s) * rows, rows, axis=0)
        total = total + swap(part, "cuts", s)
    return total


def shards(amplitudes, integrals, irrep_rows, irrep_cols, mirror_row):
    prow_count = lax.axis_size("prow")
    cuts_count = lax.axis_size("cuts")
    prow_idx = lax.axis_index("prow")
    cuts_idx = lax.axis_index("cuts")
    count = integrals.shape[0]
    labels = lax.dynamic_slice(irrep_rows, ((cuts_idx * prow_count + prow_idx) * count,), (count,))
    same = labels[:, None] == irrep_cols[None, :]
    blocked = jnp.where(same, integrals, jnp.zeros_like(integrals))
    terms = contract(amplitudes, gather_prow(blocked, prow_idx, prow_count))
    cycle = reduce_cuts(terms, cuts_idx, cuts_count)
    block_rows = cycle.shape[0]
    half = prow_count // 2
    own_block = prow_idx * cuts_count + cuts_idx
    partner_block = jnp.bitwise_xor(prow_idx, half) * cuts_count + cuts_idx
    mine = lax.dynamic_slice(mirror_row, (own_block * block_rows,), (block_rows,))
    local = mine - partner_block * block_rows
    fetched = swap(cycle, "prow", half)
    return cycle - jnp.take(fetched, local, axis=0)


def solution(mesh):
    placed = (P("prow", "cuts"), P(("cuts", "prow"), "pcol"), P(), P("pcol"), P())
    return jax.shard_map(
        shards, mesh=mesh, in_specs=placed, out_specs=P(("prow", "cuts"), "pcol"), check_vma=False
    )
```

```python
import jax
import jax.numpy as jnp
from jax import lax
from jax.experimental import pallas as pl
from jax.experimental.pallas import tpu as pltpu
from jax.sharding import PartitionSpec as P


def swap(value, axis, mask):
    return lax.ppermute(value, axis, [(i, i ^ mask) for i in range(lax.axis_size(axis))])


def gather_prow(own, prow_idx, prow_count):
    count = own.shape[0]
    if prow_count == 4 and count % 32 == 0:
        half = count // 2
        from_x = swap(own, "prow", 1)
        from_y = swap(own, "prow", 2)
        diag_a = swap(from_y[:half], "prow", 1)
        diag_b = swap(from_x[half:], "prow", 2)
        base = jnp.bitwise_xor(prow_idx, 3) * count
        return [(own, prow_idx * count), (from_x, jnp.bitwise_xor(prow_idx, 1) * count),
                (from_y, jnp.bitwise_xor(prow_idx, 2) * count), (diag_a, base), (diag_b, base + half)]
    blocks = [(own, prow_idx * count)]
    for s in range(1, prow_count):
        blocks.append((swap(own, "prow", s), jnp.bitwise_xor(prow_idx, s) * count))
    return blocks


def contract(amplitudes, blocks):
    rows, width = amplitudes.shape
    cols = blocks[0][0].shape[1]
    n = len(blocks)
    counts = [b.shape[0] for b, _ in blocks]
    if any(c % 16 for c in counts):
        piece = jnp.zeros((width, cols), blocks[0][0].dtype)
        for b, o in blocks:
            piece = lax.dynamic_update_slice(piece, b, (o, 0))
        return jnp.dot(amplitudes, piece, preferred_element_type=jnp.float32)
    offsets = jnp.stack([o for _, o in blocks]).astype(jnp.int32)
    tm = rows // 4 if rows % 32 == 0 else rows

    def kernel(off_ref, a_ref, *refs):
        w_refs = refs[:n]
        o_ref, wbuf, sem = refs[n:]

        @pl.when(pl.program_id(0) == 0)
        def _():
            copies = [pltpu.make_async_copy(w_refs[s], wbuf.at[pl.ds(pl.multiple_of(off_ref[s], 16), counts[s])], sem.at[s])
                      for s in range(n)]
            for c in copies:
                c.start()
            for c in copies:
                c.wait()

        o_ref[...] = jnp.dot(a_ref[...], wbuf[...], preferred_element_type=jnp.float32)

    grid_spec = pltpu.PrefetchScalarGridSpec(
        num_scalar_prefetch=1,
        grid=(rows // tm,),
        in_specs=[pl.BlockSpec((tm, width), lambda i, o: (i, 0))] + [pl.BlockSpec(memory_space=pl.ANY)] * n,
        out_specs=pl.BlockSpec((tm, cols), lambda i, o: (i, 0)),
        scratch_shapes=[pltpu.VMEM((width, cols), blocks[0][0].dtype), pltpu.SemaphoreType.DMA((n,))],
    )
    return pl.pallas_call(
        kernel,
        grid_spec=grid_spec,
        out_shape=jax.ShapeDtypeStruct((rows, cols), jnp.float32),
        compiler_params=pltpu.CompilerParams(dimension_semantics=("arbitrary",)),
    )(offsets, amplitudes, *[b for b, _ in blocks])


def reduce_cuts(terms, cuts_idx, cuts_count):
    rows = terms.shape[0] // cuts_count
    total = lax.dynamic_slice_in_dim(terms, cuts_idx * rows, rows, axis=0)
    for s in range(1, cuts_count):
        part = lax.dynamic_slice_in_dim(terms, jnp.bitwise_xor(cuts_idx, s) * rows, rows, axis=0)
        total = total + swap(part, "cuts", s)
    return total


def shards(amplitudes, integrals, irrep_rows, irrep_cols, mirror_row):
    prow_count = lax.axis_size("prow")
    cuts_count = lax.axis_size("cuts")
    prow_idx = lax.axis_index("prow")
    cuts_idx = lax.axis_index("cuts")
    count, cols = integrals.shape
    labels = lax.dynamic_slice(irrep_rows, ((cuts_idx * prow_count + prow_idx) * count,), (count,))
    same = labels[:, None] == irrep_cols[None, :]
    blocked = jnp.where(same, integrals, jnp.zeros_like(integrals))
    block_rows = amplitudes.shape[0] // cuts_count
    half = prow_count // 2
    own_block = prow_idx * cuts_count + cuts_idx
    partner_block = jnp.bitwise_xor(prow_idx, half) * cuts_count + cuts_idx
    mine = lax.dynamic_slice(mirror_row, (own_block * block_rows,), (block_rows,))
    local = mine - partner_block * block_rows
    chunks = 2 if cols % 16 == 0 else 1
    width = cols // chunks
    results = []
    for j in range(chunks):
        part = blocked[:, j * width:(j + 1) * width]
        terms = contract(amplitudes, gather_prow(part, prow_idx, prow_count))
        cycle = reduce_cuts(terms, cuts_idx, cuts_count)
        fetched = swap(cycle, "prow", half)
        results.append(cycle - jnp.take(fetched, local, axis=0))
    return jnp.concatenate(results, axis=1) if chunks > 1 else results[0]


def solution(mesh):
    placed = (P("prow", "cuts"), P(("cuts", "prow"), "pcol"), P(), P("pcol"), P())
    return jax.shard_map(
        shards, mesh=mesh, in_specs=placed, out_specs=P(("prow", "cuts"), "pcol"), check_vma=False
    )
```

```python
import jax
import jax.numpy as jnp
from jax import lax
from jax.experimental import pallas as pl
from jax.experimental.pallas import tpu as pltpu
from jax.sharding import PartitionSpec as P


def swap(value, axis, mask):
    return lax.ppermute(value, axis, [(i, i ^ mask) for i in range(lax.axis_size(axis))])


def gather_prow(own, prow_idx, prow_count):
    count = own.shape[0]
    if prow_count == 4 and count % 32 == 0:
        half = count // 2
        from_x = swap(own, "prow", 1)
        from_y = swap(own, "prow", 2)
        diag_a = swap(from_y[:half], "prow", 1)
        diag_b = swap(from_x[half:], "prow", 2)
        base = jnp.bitwise_xor(prow_idx, 3) * count
        return [(own, prow_idx * count), (from_x, jnp.bitwise_xor(prow_idx, 1) * count),
                (from_y, jnp.bitwise_xor(prow_idx, 2) * count), (diag_a, base), (diag_b, base + half)]
    blocks = [(own, prow_idx * count)]
    for s in range(1, prow_count):
        blocks.append((swap(own, "prow", s), jnp.bitwise_xor(prow_idx, s) * count))
    return blocks


def assemble(blocks, width):
    cols = blocks[0][0].shape[1]
    dtype = blocks[0][0].dtype
    n = len(blocks)
    counts = [b.shape[0] for b, _ in blocks]
    if any(c % 16 for c in counts):
        piece = jnp.zeros((width, cols), dtype)
        for b, o in blocks:
            piece = lax.dynamic_update_slice(piece, b, (o, 0))
        return piece
    offsets = jnp.stack([o for _, o in blocks]).astype(jnp.int32)

    def kernel(off_ref, *refs):
        w_refs = refs[:n]
        o_ref, sem = refs[n:]
        copies = [pltpu.make_async_copy(w_refs[s], o_ref.at[pl.ds(pl.multiple_of(off_ref[s], 16), counts[s])], sem.at[s])
                  for s in range(n)]
        for c in copies:
            c.start()
        for c in copies:
            c.wait()

    grid_spec = pltpu.PrefetchScalarGridSpec(
        num_scalar_prefetch=1,
        grid=(1,),
        in_specs=[pl.BlockSpec(memory_space=pl.ANY)] * n,
        out_specs=pl.BlockSpec(memory_space=pl.ANY),
        scratch_shapes=[pltpu.SemaphoreType.DMA((n,))],
    )
    return pl.pallas_call(
        kernel, grid_spec=grid_spec, out_shape=jax.ShapeDtypeStruct((width, cols), dtype)
    )(offsets, *[b for b, _ in blocks])


def contract(amplitudes, blocks):
    piece = assemble(blocks, amplitudes.shape[1])
    return jnp.dot(amplitudes, piece, preferred_element_type=jnp.float32)


def reduce_cuts(terms, cuts_idx, cuts_count):
    rows = terms.shape[0] // cuts_count
    total = lax.dynamic_slice_in_dim(terms, cuts_idx * rows, rows, axis=0)
    for s in range(1, cuts_count):
        part = lax.dynamic_slice_in_dim(terms, jnp.bitwise_xor(cuts_idx, s) * rows, rows, axis=0)
        total = total + swap(part, "cuts", s)
    return total


def shards(amplitudes, integrals, irrep_rows, irrep_cols, mirror_row):
    prow_count = lax.axis_size("prow")
    cuts_count = lax.axis_size("cuts")
    prow_idx = lax.axis_index("prow")
    cuts_idx = lax.axis_index("cuts")
    count, cols = integrals.shape
    labels = lax.dynamic_slice(irrep_rows, ((cuts_idx * prow_count + prow_idx) * count,), (count,))
    same = labels[:, None] == irrep_cols[None, :]
    blocked = jnp.where(same, integrals, jnp.zeros_like(integrals))
    block_rows = amplitudes.shape[0] // cuts_count
    half = prow_count // 2
    own_block = prow_idx * cuts_count + cuts_idx
    partner_block = jnp.bitwise_xor(prow_idx, half) * cuts_count + cuts_idx
    mine = lax.dynamic_slice(mirror_row, (own_block * block_rows,), (block_rows,))
    local = mine - partner_block * block_rows
    chunks = 2 if cols % 16 == 0 else 1
    width = cols // chunks
    results = []
    for j in range(chunks):
        part = blocked[:, j * width:(j + 1) * width]
        terms = contract(amplitudes, gather_prow(part, prow_idx, prow_count))
        cycle = reduce_cuts(terms, cuts_idx, cuts_count)
        fetched = swap(cycle, "prow", half)
        results.append(cycle - jnp.take(fetched, local, axis=0))
    return jnp.concatenate(results, axis=1) if chunks > 1 else results[0]


def solution(mesh):
    placed = (P("prow", "cuts"), P(("cuts", "prow"), "pcol"), P(), P("pcol"), P())
    return jax.shard_map(
        shards, mesh=mesh, in_specs=placed, out_specs=P(("prow", "cuts"), "pcol"), check_vma=False
    )
```

```python
import jax
import jax.numpy as jnp
from jax import lax
from jax.experimental import pallas as pl
from jax.experimental.pallas import tpu as pltpu
from jax.sharding import PartitionSpec as P


def swap(value, axis, mask):
    return lax.ppermute(value, axis, [(i, i ^ mask) for i in range(lax.axis_size(axis))])


def gather_prow(own, prow_idx, prow_count):
    count = own.shape[0]
    if prow_count == 4 and count % 32 == 0:
        half = count // 2
        from_x = swap(own, "prow", 1)
        from_y = swap(own, "prow", 2)
        diag_a = swap(from_y[:half], "prow", 1)
        diag_b = swap(from_x[half:], "prow", 2)
        base = jnp.bitwise_xor(prow_idx, 3) * count
        return [[(own, prow_idx * count)], [(from_y, jnp.bitwise_xor(prow_idx, 2) * count)],
                [(from_x, jnp.bitwise_xor(prow_idx, 1) * count)], [(diag_a, base), (diag_b, base + half)]]
    groups = [[(own, prow_idx * count)]]
    for s in range(1, prow_count):
        groups.append([(swap(own, "prow", s), jnp.bitwise_xor(prow_idx, s) * count)])
    return groups


def window(count, width, prow_count):
    lane = 128
    if width % lane or count % 16:
        return None
    span = max(-(-((j * count) % lane + count) // lane) * lane for j in range(prow_count))
    if any((j * count) // lane * lane + span > width for j in range(prow_count)):
        return None
    return span


def partial_product(amplitudes, group, first, span, acc):
    rows, width = amplitudes.shape
    cols = group[0][0].shape[1]
    lane = 128
    n = len(group)
    counts = [b.shape[0] for b, _ in group]
    offsets = jnp.stack([first] + [o - first // lane * lane for _, o in group]).astype(jnp.int32)

    def kernel(off_ref, a_hbm, *refs):
        w_refs = refs[:n]
        rest = refs[n:]
        if acc is None:
            o_ref, a_buf, w_buf, sem = rest
        else:
            acc_ref, o_ref, a_buf, w_buf, sem = rest
        start = pl.multiple_of(off_ref[0] // lane * lane, lane)
        copy = pltpu.make_async_copy(a_hbm.at[:, pl.ds(start, span)], a_buf, sem.at[0])
        copy.start()
        w_buf[...] = jnp.zeros(w_buf.shape, w_buf.dtype)
        for s in range(n):
            w_buf[pl.ds(pl.multiple_of(off_ref[s + 1], 16), counts[s]), :] = w_refs[s][...]
        copy.wait()
        product = jnp.dot(a_buf[...], w_buf[...], preferred_element_type=jnp.float32)
        o_ref[...] = product if acc is None else acc_ref[...] + product

    vmem = pl.BlockSpec(memory_space=pltpu.MemorySpace.VMEM)
    smem = pl.BlockSpec(memory_space=pltpu.MemorySpace.SMEM)
    operands = [offsets, amplitudes] + [b for b, _ in group] + ([] if acc is None else [acc])
    return pl.pallas_call(
        kernel,
        in_specs=[smem, pl.BlockSpec(memory_space=pl.ANY)] + [vmem] * (len(operands) - 2),
        out_specs=vmem,
        out_shape=jax.ShapeDtypeStruct((rows, cols), jnp.float32),
        scratch_shapes=[pltpu.VMEM((rows, span), amplitudes.dtype), pltpu.VMEM((span, cols), group[0][0].dtype),
                        pltpu.SemaphoreType.DMA((1,))],
        input_output_aliases={} if acc is None else {len(operands) - 1: 0},
    )(*operands)


def contract(amplitudes, groups, prow_idx, prow_count):
    rows, width = amplitudes.shape
    count, cols = groups[0][0][0].shape
    span = window(count, width, prow_count)
    if span is None:
        piece = jnp.zeros((width, cols), groups[0][0][0].dtype)
        for group in groups:
            for b, o in group:
                piece = lax.dynamic_update_slice(piece, b, (o, 0))
        return jnp.dot(amplitudes, piece, preferred_element_type=jnp.float32)
    acc = None
    for group in groups:
        acc = partial_product(amplitudes, group, group[0][1], span, acc)
    return acc


def reduce_cuts(terms, cuts_idx, cuts_count):
    rows = terms.shape[0] // cuts_count
    total = lax.dynamic_slice_in_dim(terms, cuts_idx * rows, rows, axis=0)
    for s in range(1, cuts_count):
        part = lax.dynamic_slice_in_dim(terms, jnp.bitwise_xor(cuts_idx, s) * rows, rows, axis=0)
        total = total + swap(part, "cuts", s)
    return total


def shards(amplitudes, integrals, irrep_rows, irrep_cols, mirror_row):
    prow_count = lax.axis_size("prow")
    cuts_count = lax.axis_size("cuts")
    prow_idx = lax.axis_index("prow")
    cuts_idx = lax.axis_index("cuts")
    count = integrals.shape[0]
    labels = lax.dynamic_slice(irrep_rows, ((cuts_idx * prow_count + prow_idx) * count,), (count,))
    same = labels[:, None] == irrep_cols[None, :]
    blocked = jnp.where(same, integrals, jnp.zeros_like(integrals))
    terms = contract(amplitudes, gather_prow(blocked, prow_idx, prow_count), prow_idx, prow_count)
    cycle = reduce_cuts(terms, cuts_idx, cuts_count)
    block_rows = cycle.shape[0]
    half = prow_count // 2
    own_block = prow_idx * cuts_count + cuts_idx
    partner_block = jnp.bitwise_xor(prow_idx, half) * cuts_count + cuts_idx
    mine = lax.dynamic_slice(mirror_row, (own_block * block_rows,), (block_rows,))
    local = mine - partner_block * block_rows
    fetched = swap(cycle, "prow", half)
    return cycle - jnp.take(fetched, local, axis=0)


def solution(mesh):
    placed = (P("prow", "cuts"), P(("cuts", "prow"), "pcol"), P(), P("pcol"), P())
    return jax.shard_map(
        shards, mesh=mesh, in_specs=placed, out_specs=P(("prow", "cuts"), "pcol"), check_vma=False
    )
```

```python
import jax
import jax.numpy as jnp
from jax import lax
from jax.experimental import pallas as pl
from jax.experimental.pallas import tpu as pltpu
from jax.sharding import PartitionSpec as P


def swap(value, axis, mask):
    return lax.ppermute(value, axis, [(i, i ^ mask) for i in range(lax.axis_size(axis))])


def gather_prow(own, prow_idx, prow_count):
    count = own.shape[0]
    if prow_count == 4 and count % 32 == 0:
        half = count // 2
        from_x = swap(own, "prow", 1)
        from_y = swap(own, "prow", 2)
        diag_a = swap(from_y[:half], "prow", 1)
        diag_b = swap(from_x[half:], "prow", 2)
        base = jnp.bitwise_xor(prow_idx, 3) * count
        return [[(own, prow_idx * count)], [(from_y, jnp.bitwise_xor(prow_idx, 2) * count)],
                [(from_x, jnp.bitwise_xor(prow_idx, 1) * count)], [(diag_a, base), (diag_b, base + half)]]
    groups = [[(own, prow_idx * count)]]
    for s in range(1, prow_count):
        groups.append([(swap(own, "prow", s), jnp.bitwise_xor(prow_idx, s) * count)])
    return groups


def contract(amplitudes, groups, prow_idx, prow_count):
    terms = None
    for group in groups:
        for b, o in group:
            window = lax.dynamic_slice_in_dim(amplitudes, o, b.shape[0], axis=1)
            product = jnp.dot(window, b, preferred_element_type=jnp.float32)
            terms = product if terms is None else terms + product
    return terms


def reduce_cuts(terms, cuts_idx, cuts_count):
    rows = terms.shape[0] // cuts_count
    total = lax.dynamic_slice_in_dim(terms, cuts_idx * rows, rows, axis=0)
    for s in range(1, cuts_count):
        part = lax.dynamic_slice_in_dim(terms, jnp.bitwise_xor(cuts_idx, s) * rows, rows, axis=0)
        total = total + swap(part, "cuts", s)
    return total


def shards(amplitudes, integrals, irrep_rows, irrep_cols, mirror_row):
    prow_count = lax.axis_size("prow")
    cuts_count = lax.axis_size("cuts")
    prow_idx = lax.axis_index("prow")
    cuts_idx = lax.axis_index("cuts")
    count = integrals.shape[0]
    labels = lax.dynamic_slice(irrep_rows, ((cuts_idx * prow_count + prow_idx) * count,), (count,))
    same = labels[:, None] == irrep_cols[None, :]
    blocked = jnp.where(same, integrals, jnp.zeros_like(integrals))
    terms = contract(amplitudes, gather_prow(blocked, prow_idx, prow_count), prow_idx, prow_count)
    cycle = reduce_cuts(terms, cuts_idx, cuts_count)
    block_rows = cycle.shape[0]
    half = prow_count // 2
    own_block = prow_idx * cuts_count + cuts_idx
    partner_block = jnp.bitwise_xor(prow_idx, half) * cuts_count + cuts_idx
    mine = lax.dynamic_slice(mirror_row, (own_block * block_rows,), (block_rows,))
    local = mine - partner_block * block_rows
    fetched = swap(cycle, "prow", half)
    return cycle - jnp.take(fetched, local, axis=0)


def solution(mesh):
    placed = (P("prow", "cuts"), P(("cuts", "prow"), "pcol"), P(), P("pcol"), P())
    return jax.shard_map(
        shards, mesh=mesh, in_specs=placed, out_specs=P(("prow", "cuts"), "pcol"), check_vma=False
    )
```

```python
import jax
import jax.numpy as jnp
from jax import lax
from jax.experimental import pallas as pl
from jax.experimental.pallas import tpu as pltpu
from jax.sharding import PartitionSpec as P


def swap(value, axis, mask):
    return lax.ppermute(value, axis, [(i, i ^ mask) for i in range(lax.axis_size(axis))])


def gather_prow(own, prow_idx, prow_count):
    count = own.shape[0]
    if prow_count == 4 and count % 32 == 0:
        half = count // 2
        from_x = swap(own, "prow", 1)
        from_y = swap(own, "prow", 2)
        diag_a = swap(from_y[:half], "prow", 1)
        diag_b = swap(from_x[half:], "prow", 2)
        base = jnp.bitwise_xor(prow_idx, 3) * count
        return [[(own, prow_idx * count)], [(from_y, jnp.bitwise_xor(prow_idx, 2) * count)],
                [(from_x, jnp.bitwise_xor(prow_idx, 1) * count)], [(diag_a, base), (diag_b, base + half)]]
    groups = [[(own, prow_idx * count)]]
    for s in range(1, prow_count):
        groups.append([(swap(own, "prow", s), jnp.bitwise_xor(prow_idx, s) * count)])
    return groups


def contract(amplitudes, groups, first, rows):
    band = lax.dynamic_slice_in_dim(amplitudes, first, rows, axis=0)
    terms = None
    for group in groups:
        for b, o in group:
            window = lax.dynamic_slice_in_dim(band, o, b.shape[0], axis=1)
            product = jnp.dot(window, b, preferred_element_type=jnp.float32)
            terms = product if terms is None else terms + product
    return terms


def shards(amplitudes, integrals, irrep_rows, irrep_cols, mirror_row):
    prow_count = lax.axis_size("prow")
    cuts_count = lax.axis_size("cuts")
    prow_idx = lax.axis_index("prow")
    cuts_idx = lax.axis_index("cuts")
    count = integrals.shape[0]
    labels = lax.dynamic_slice(irrep_rows, ((cuts_idx * prow_count + prow_idx) * count,), (count,))
    same = labels[:, None] == irrep_cols[None, :]
    blocked = jnp.where(same, integrals, jnp.zeros_like(integrals))
    groups = gather_prow(blocked, prow_idx, prow_count)
    block_rows = amplitudes.shape[0] // cuts_count
    sent = []
    for s in range(1, cuts_count):
        other = jnp.bitwise_xor(cuts_idx, s)
        sent.append((s, contract(amplitudes, groups, other * block_rows, block_rows)))
    kept = contract(amplitudes, groups, cuts_idx * block_rows, block_rows)
    pieces = 2 if block_rows % 16 == 0 else 1
    step = block_rows // pieces
    half = prow_count // 2
    fetched = []
    cycle = []
    for h in range(pieces):
        total = kept[h * step:(h + 1) * step]
        for s, part in sent:
            total = total + swap(part[h * step:(h + 1) * step], "cuts", s)
        cycle.append(total)
        fetched.append(swap(total, "prow", half))
    cycle = jnp.concatenate(cycle, axis=0) if pieces > 1 else cycle[0]
    fetched = jnp.concatenate(fetched, axis=0) if pieces > 1 else fetched[0]
    own_block = prow_idx * cuts_count + cuts_idx
    partner_block = jnp.bitwise_xor(prow_idx, half) * cuts_count + cuts_idx
    mine = lax.dynamic_slice(mirror_row, (own_block * block_rows,), (block_rows,))
    local = mine - partner_block * block_rows
    return cycle - jnp.take(fetched, local, axis=0, mode="clip")


def solution(mesh):
    placed = (P("prow", "cuts"), P(("cuts", "prow"), "pcol"), P(), P("pcol"), P())
    return jax.shard_map(
        shards, mesh=mesh, in_specs=placed, out_specs=P(("prow", "cuts"), "pcol"), check_vma=False
    )
```

```python
import jax
import jax.numpy as jnp
from jax import lax
from jax.experimental import pallas as pl
from jax.experimental.pallas import tpu as pltpu
from jax.sharding import PartitionSpec as P


def swap(value, axis, mask):
    return lax.ppermute(value, axis, [(i, i ^ mask) for i in range(lax.axis_size(axis))])


def gather_prow(own, prow_idx, prow_count):
    count = own.shape[0]
    if prow_count == 4 and count % 32 == 0:
        half = count // 2
        from_x = swap(own, "prow", 1)
        from_y = swap(own, "prow", 2)
        diag_a = swap(from_y[:half], "prow", 1)
        diag_b = swap(from_x[half:], "prow", 2)
        base = jnp.bitwise_xor(prow_idx, 3) * count
        return [[(own, prow_idx * count)], [(from_y, jnp.bitwise_xor(prow_idx, 2) * count)],
                [(from_x, jnp.bitwise_xor(prow_idx, 1) * count)], [(diag_a, base), (diag_b, base + half)]]
    groups = [[(own, prow_idx * count)]]
    for s in range(1, prow_count):
        groups.append([(swap(own, "prow", s), jnp.bitwise_xor(prow_idx, s) * count)])
    return groups


def contract(amplitudes, groups, first, rows, labels, irrep_cols):
    band = lax.dynamic_slice_in_dim(amplitudes, first, rows, axis=0)
    terms = None
    for group in groups:
        for b, o in group:
            window = lax.dynamic_slice_in_dim(band, o, b.shape[0], axis=1)
            same = lax.dynamic_slice_in_dim(labels, o, b.shape[0])[:, None] == irrep_cols[None, :]
            blocked = jnp.where(same, b, jnp.zeros_like(b))
            product = jnp.dot(window, blocked, preferred_element_type=jnp.float32)
            terms = product if terms is None else terms + product
    return terms


def shards(amplitudes, integrals, irrep_rows, irrep_cols, mirror_row):
    prow_count = lax.axis_size("prow")
    cuts_count = lax.axis_size("cuts")
    prow_idx = lax.axis_index("prow")
    cuts_idx = lax.axis_index("cuts")
    width = amplitudes.shape[1]
    labels = lax.dynamic_slice_in_dim(irrep_rows, cuts_idx * width, width)
    groups = gather_prow(integrals, prow_idx, prow_count)
    block_rows = amplitudes.shape[0] // cuts_count
    sent = []
    for s in range(1, cuts_count):
        other = jnp.bitwise_xor(cuts_idx, s)
        sent.append((s, contract(amplitudes, groups, other * block_rows, block_rows, labels, irrep_cols)))
    kept = contract(amplitudes, groups, cuts_idx * block_rows, block_rows, labels, irrep_cols)
    pieces = 2 if block_rows % 16 == 0 else 1
    step = block_rows // pieces
    half = prow_count // 2
    fetched = []
    cycle = []
    for h in range(pieces):
        total = kept[h * step:(h + 1) * step]
        for s, part in sent:
            total = total + swap(part[h * step:(h + 1) * step], "cuts", s)
        cycle.append(total)
        fetched.append(swap(total, "prow", half))
    cycle = jnp.concatenate(cycle, axis=0) if pieces > 1 else cycle[0]
    fetched = jnp.concatenate(fetched, axis=0) if pieces > 1 else fetched[0]
    own_block = prow_idx * cuts_count + cuts_idx
    partner_block = jnp.bitwise_xor(prow_idx, half) * cuts_count + cuts_idx
    mine = lax.dynamic_slice(mirror_row, (own_block * block_rows,), (block_rows,))
    local = mine - partner_block * block_rows
    return cycle - jnp.take(fetched, local, axis=0, mode="clip")


def solution(mesh):
    placed = (P("prow", "cuts"), P(("cuts", "prow"), "pcol"), P(), P("pcol"), P())
    return jax.shard_map(
        shards, mesh=mesh, in_specs=placed, out_specs=P(("prow", "cuts"), "pcol"), check_vma=False
    )
```

```python
import jax
import jax.numpy as jnp
from jax import lax
from jax.experimental import pallas as pl
from jax.experimental.pallas import tpu as pltpu
from jax.sharding import PartitionSpec as P


def swap(value, axis, mask):
    return lax.ppermute(value, axis, [(i, i ^ mask) for i in range(lax.axis_size(axis))])


def gather_prow(own, prow_idx, prow_count, via_x=False, hold=None):
    count = own.shape[0]
    if prow_count == 4 and count % 32 == 0:
        half = count // 2
        from_x = swap(own, "prow", 1)
        from_y = swap(own, "prow", 2)
        if hold is not None:
            from_x, from_y, _ = lax.optimization_barrier((from_x, from_y, hold))
        if via_x:
            return [[(own, prow_idx * count)], [(from_y, jnp.bitwise_xor(prow_idx, 2) * count)],
                    [(from_x, jnp.bitwise_xor(prow_idx, 1) * count)],
                    [(swap(from_y, "prow", 1), jnp.bitwise_xor(prow_idx, 3) * count)]]
        diag_a = swap(from_y[:half], "prow", 1)
        diag_b = swap(from_x[half:], "prow", 2)
        base = jnp.bitwise_xor(prow_idx, 3) * count
        return [[(own, prow_idx * count)], [(from_y, jnp.bitwise_xor(prow_idx, 2) * count)],
                [(from_x, jnp.bitwise_xor(prow_idx, 1) * count)], [(diag_a, base), (diag_b, base + half)]]
    groups = [[(own, prow_idx * count)]]
    for s in range(1, prow_count):
        groups.append([(swap(own, "prow", s), jnp.bitwise_xor(prow_idx, s) * count)])
    return groups


def contract(amplitudes, groups, first, rows, labels, irrep_cols):
    band = lax.dynamic_slice_in_dim(amplitudes, first, rows, axis=0)
    terms = None
    for group in groups:
        for b, o in group:
            window = lax.dynamic_slice_in_dim(band, o, b.shape[0], axis=1)
            same = lax.dynamic_slice_in_dim(labels, o, b.shape[0])[:, None] == irrep_cols[None, :]
            blocked = jnp.where(same, b, jnp.zeros_like(b))
            product = jnp.dot(window, blocked, preferred_element_type=jnp.float32)
            terms = product if terms is None else terms + product
    return terms


def antisym(amplitudes, integrals, labels, irrep_cols, local, via_x, pieces, after, hold):
    prow_count = lax.axis_size("prow")
    cuts_count = lax.axis_size("cuts")
    prow_idx = lax.axis_index("prow")
    cuts_idx = lax.axis_index("cuts")
    if after is not None:
        integrals, _ = lax.optimization_barrier((integrals, after))
    groups = gather_prow(integrals, prow_idx, prow_count, via_x, hold)
    block_rows = amplitudes.shape[0] // cuts_count
    sent = []
    for s in range(1, cuts_count):
        other = jnp.bitwise_xor(cuts_idx, s)
        sent.append((s, contract(amplitudes, groups, other * block_rows, block_rows, labels, irrep_cols)))
    kept = contract(amplitudes, groups, cuts_idx * block_rows, block_rows, labels, irrep_cols)
    pieces = pieces if block_rows % (8 * pieces) == 0 else 1
    step = block_rows // pieces
    half = prow_count // 2
    fetched = []
    cycle = []
    for h in range(pieces):
        total = kept[h * step:(h + 1) * step]
        for s, part in sent:
            total = total + swap(part[h * step:(h + 1) * step], "cuts", s)
        cycle.append(total)
        fetched.append(swap(total, "prow", half))
    cycle = jnp.concatenate(cycle, axis=0) if pieces > 1 else cycle[0]
    fetched = jnp.concatenate(fetched, axis=0) if pieces > 1 else fetched[0]
    return cycle - jnp.take(fetched, local, axis=0, mode="clip"), groups[1][0][0], cycle


def shards(amplitudes, integrals, irrep_rows, irrep_cols, mirror_row):
    prow_count = lax.axis_size("prow")
    cuts_count = lax.axis_size("cuts")
    prow_idx = lax.axis_index("prow")
    cuts_idx = lax.axis_index("cuts")
    width = amplitudes.shape[1]
    cols = integrals.shape[1]
    labels = lax.dynamic_slice_in_dim(irrep_rows, cuts_idx * width, width)
    block_rows = amplitudes.shape[0] // cuts_count
    half = prow_count // 2
    own_block = prow_idx * cuts_count + cuts_idx
    partner_block = jnp.bitwise_xor(prow_idx, half) * cuts_count + cuts_idx
    mine = lax.dynamic_slice(mirror_row, (own_block * block_rows,), (block_rows,))
    local = mine - partner_block * block_rows
    chunks = 2 if cols % 16 == 0 else 1
    step = cols // chunks
    results = []
    after = None
    hold = None
    for j in range(chunks):
        result, after, hold = antisym(amplitudes, integrals[:, j * step:(j + 1) * step], labels,
                                      irrep_cols[j * step:(j + 1) * step], local, False, 1 if chunks > 1 else 2,
                                      after, hold)
        results.append(result)
    return jnp.concatenate(results, axis=1) if chunks > 1 else results[0]


def solution(mesh):
    placed = (P("prow", "cuts"), P(("cuts", "prow"), "pcol"), P(), P("pcol"), P())
    return jax.shard_map(
        shards, mesh=mesh, in_specs=placed, out_specs=P(("prow", "cuts"), "pcol"), check_vma=False
    )
```

```python
import jax
import jax.numpy as jnp
from jax import lax
from jax.experimental import pallas as pl
from jax.experimental.pallas import tpu as pltpu
from jax.sharding import PartitionSpec as P


def swap(value, axis, mask):
    return lax.ppermute(value, axis, [(i, i ^ mask) for i in range(lax.axis_size(axis))])


def gather_prow(own, prow_idx, prow_count, via_x=False, hold=None):
    count = own.shape[0]
    if prow_count == 4 and count % 32 == 0:
        half = count // 2
        from_x = swap(own, "prow", 1)
        from_y = swap(own, "prow", 2)
        if hold is not None:
            from_x, from_y, _ = lax.optimization_barrier((from_x, from_y, hold))
        if via_x:
            return [[(own, prow_idx * count)], [(from_y, jnp.bitwise_xor(prow_idx, 2) * count)],
                    [(from_x, jnp.bitwise_xor(prow_idx, 1) * count)],
                    [(swap(from_y, "prow", 1), jnp.bitwise_xor(prow_idx, 3) * count)]]
        diag_a = swap(from_y[:half], "prow", 1)
        diag_b = swap(from_x[half:], "prow", 2)
        base = jnp.bitwise_xor(prow_idx, 3) * count
        return [[(own, prow_idx * count)], [(from_y, jnp.bitwise_xor(prow_idx, 2) * count)],
                [(from_x, jnp.bitwise_xor(prow_idx, 1) * count)], [(diag_a, base), (diag_b, base + half)]]
    groups = [[(own, prow_idx * count)]]
    for s in range(1, prow_count):
        groups.append([(swap(own, "prow", s), jnp.bitwise_xor(prow_idx, s) * count)])
    return groups


def contract(amplitudes, groups, first, rows, labels, irrep_cols):
    band = lax.dynamic_slice_in_dim(amplitudes, first, rows, axis=0)
    terms = None
    for group in groups:
        for b, o in group:
            window = lax.dynamic_slice_in_dim(band, o, b.shape[0], axis=1)
            same = lax.dynamic_slice_in_dim(labels, o, b.shape[0])[:, None] == irrep_cols[None, :]
            blocked = jnp.where(same, b, jnp.zeros_like(b))
            product = jnp.dot(window, blocked, preferred_element_type=jnp.float32)
            terms = product if terms is None else terms + product
    return terms


def antisym(amplitudes, integrals, labels, irrep_cols, local, via_x, pieces, after, hold):
    prow_count = lax.axis_size("prow")
    cuts_count = lax.axis_size("cuts")
    prow_idx = lax.axis_index("prow")
    cuts_idx = lax.axis_index("cuts")
    if after is not None:
        integrals, _ = lax.optimization_barrier((integrals, after))
    groups = gather_prow(integrals, prow_idx, prow_count, via_x, hold)
    block_rows = amplitudes.shape[0] // cuts_count
    sent = []
    for s in range(1, cuts_count):
        other = jnp.bitwise_xor(cuts_idx, s)
        sent.append((s, contract(amplitudes, groups, other * block_rows, block_rows, labels, irrep_cols)))
    kept = contract(amplitudes, groups, cuts_idx * block_rows, block_rows, labels, irrep_cols)
    pieces = pieces if block_rows % (8 * pieces) == 0 else 1
    step = block_rows // pieces
    half = prow_count // 2
    fetched = []
    cycle = []
    for h in range(pieces):
        total = kept[h * step:(h + 1) * step]
        for s, part in sent:
            total = total + swap(part[h * step:(h + 1) * step], "cuts", s)
        cycle.append(total)
        fetched.append(swap(total, "prow", half))
    cycle = jnp.concatenate(cycle, axis=0) if pieces > 1 else cycle[0]
    fetched = jnp.concatenate(fetched, axis=0) if pieces > 1 else fetched[0]
    return cycle - jnp.take(fetched, local, axis=0, mode="clip"), groups[1][0][0], cycle


def shards(amplitudes, integrals, irrep_rows, irrep_cols, mirror_row):
    prow_count = lax.axis_size("prow")
    cuts_count = lax.axis_size("cuts")
    prow_idx = lax.axis_index("prow")
    cuts_idx = lax.axis_index("cuts")
    width = amplitudes.shape[1]
    cols = integrals.shape[1]
    labels = lax.dynamic_slice_in_dim(irrep_rows, cuts_idx * width, width)
    block_rows = amplitudes.shape[0] // cuts_count
    half = prow_count // 2
    own_block = prow_idx * cuts_count + cuts_idx
    partner_block = jnp.bitwise_xor(prow_idx, half) * cuts_count + cuts_idx
    mine = lax.dynamic_slice(mirror_row, (own_block * block_rows,), (block_rows,))
    local = mine - partner_block * block_rows
    chunks = 2 if cols % 16 == 0 else 1
    step = cols // chunks
    results = []
    after = None
    hold = None
    for j in range(chunks):
        result, after, hold = antisym(amplitudes, integrals[:, j * step:(j + 1) * step], labels,
                                      irrep_cols[j * step:(j + 1) * step], local, chunks > 1, 1 if chunks > 1 else 2,
                                      after, hold)
        results.append(result)
    return jnp.concatenate(results, axis=1) if chunks > 1 else results[0]


def solution(mesh):
    placed = (P("prow", "cuts"), P(("cuts", "prow"), "pcol"), P(), P("pcol"), P())
    return jax.shard_map(
        shards, mesh=mesh, in_specs=placed, out_specs=P(("prow", "cuts"), "pcol"), check_vma=False
    )
```

```python
import jax
import jax.numpy as jnp
from jax import lax
from jax.experimental import pallas as pl
from jax.experimental.pallas import tpu as pltpu
from jax.sharding import PartitionSpec as P


def swap(value, axis, mask):
    return lax.ppermute(value, axis, [(i, i ^ mask) for i in range(lax.axis_size(axis))])


def gather_prow(own, prow_idx, prow_count, via_x=False, hold=None):
    count = own.shape[0]
    if prow_count == 4 and count % 32 == 0:
        half = count // 2
        from_x = swap(own, "prow", 1)
        from_y = swap(own, "prow", 2)
        if hold is not None:
            from_x, from_y, _ = lax.optimization_barrier((from_x, from_y, hold))
        if via_x:
            return [[(own, prow_idx * count)], [(from_y, jnp.bitwise_xor(prow_idx, 2) * count)],
                    [(from_x, jnp.bitwise_xor(prow_idx, 1) * count)],
                    [(swap(from_y, "prow", 1), jnp.bitwise_xor(prow_idx, 3) * count)]]
        diag_a = swap(from_y[:half], "prow", 1)
        diag_b = swap(from_x[half:], "prow", 2)
        base = jnp.bitwise_xor(prow_idx, 3) * count
        return [[(own, prow_idx * count)], [(from_y, jnp.bitwise_xor(prow_idx, 2) * count)],
                [(from_x, jnp.bitwise_xor(prow_idx, 1) * count)], [(diag_a, base), (diag_b, base + half)]]
    groups = [[(own, prow_idx * count)]]
    for s in range(1, prow_count):
        groups.append([(swap(own, "prow", s), jnp.bitwise_xor(prow_idx, s) * count)])
    return groups


def contract(amplitudes, groups, first, rows, labels, irrep_cols):
    band = lax.dynamic_slice_in_dim(amplitudes, first, rows, axis=0)
    terms = None
    for group in groups:
        for b, o in group:
            window = lax.dynamic_slice_in_dim(band, o, b.shape[0], axis=1)
            same = lax.dynamic_slice_in_dim(labels, o, b.shape[0])[:, None] == irrep_cols[None, :]
            blocked = jnp.where(same, b, jnp.zeros_like(b))
            product = jnp.dot(window, blocked, preferred_element_type=jnp.float32)
            terms = product if terms is None else terms + product
    return terms


def antisym(amplitudes, integrals, labels, irrep_cols, local, via_x, pieces, after, hold):
    prow_count = lax.axis_size("prow")
    cuts_count = lax.axis_size("cuts")
    prow_idx = lax.axis_index("prow")
    cuts_idx = lax.axis_index("cuts")
    if after is not None:
        integrals, _ = lax.optimization_barrier((integrals, after))
    groups = gather_prow(integrals, prow_idx, prow_count, via_x, hold)
    block_rows = amplitudes.shape[0] // cuts_count
    sent = []
    if via_x:
        terms = contract(amplitudes, groups, 0, amplitudes.shape[0], labels, irrep_cols)
        for s in range(1, cuts_count):
            other = jnp.bitwise_xor(cuts_idx, s)
            sent.append((s, lax.dynamic_slice_in_dim(terms, other * block_rows, block_rows)))
        kept = lax.dynamic_slice_in_dim(terms, cuts_idx * block_rows, block_rows)
    else:
        for s in range(1, cuts_count):
            other = jnp.bitwise_xor(cuts_idx, s)
            sent.append((s, contract(amplitudes, groups, other * block_rows, block_rows, labels, irrep_cols)))
        kept = contract(amplitudes, groups, cuts_idx * block_rows, block_rows, labels, irrep_cols)
    pieces = pieces if block_rows % (8 * pieces) == 0 else 1
    step = block_rows // pieces
    half = prow_count // 2
    fetched = []
    cycle = []
    for h in range(pieces):
        total = kept[h * step:(h + 1) * step]
        for s, part in sent:
            total = total + swap(part[h * step:(h + 1) * step], "cuts", s)
        cycle.append(total)
        fetched.append(swap(total, "prow", half))
    cycle = jnp.concatenate(cycle, axis=0) if pieces > 1 else cycle[0]
    fetched = jnp.concatenate(fetched, axis=0) if pieces > 1 else fetched[0]
    return cycle - jnp.take(fetched, local, axis=0, mode="clip"), groups[1][0][0], cycle


def shards(amplitudes, integrals, irrep_rows, irrep_cols, mirror_row):
    prow_count = lax.axis_size("prow")
    cuts_count = lax.axis_size("cuts")
    prow_idx = lax.axis_index("prow")
    cuts_idx = lax.axis_index("cuts")
    width = amplitudes.shape[1]
    cols = integrals.shape[1]
    labels = lax.dynamic_slice_in_dim(irrep_rows, cuts_idx * width, width)
    block_rows = amplitudes.shape[0] // cuts_count
    half = prow_count // 2
    own_block = prow_idx * cuts_count + cuts_idx
    partner_block = jnp.bitwise_xor(prow_idx, half) * cuts_count + cuts_idx
    mine = lax.dynamic_slice(mirror_row, (own_block * block_rows,), (block_rows,))
    local = mine - partner_block * block_rows
    chunks = 2 if cols % 16 == 0 else 1
    step = cols // chunks
    results = []
    after = None
    hold = None
    for j in range(chunks):
        result, after, hold = antisym(amplitudes, integrals[:, j * step:(j + 1) * step], labels,
                                      irrep_cols[j * step:(j + 1) * step], local, chunks > 1, 1 if chunks > 1 else 2,
                                      after, hold)
        results.append(result)
    return jnp.concatenate(results, axis=1) if chunks > 1 else results[0]


def solution(mesh):
    placed = (P("prow", "cuts"), P(("cuts", "prow"), "pcol"), P(), P("pcol"), P())
    return jax.shard_map(
        shards, mesh=mesh, in_specs=placed, out_specs=P(("prow", "cuts"), "pcol"), check_vma=False
    )
```

```python
import jax
import jax.numpy as jnp
from jax import lax
from jax.experimental import pallas as pl
from jax.experimental.pallas import tpu as pltpu
from jax.sharding import PartitionSpec as P


def swap(value, axis, mask):
    return lax.ppermute(value, axis, [(i, i ^ mask) for i in range(lax.axis_size(axis))])


def gather_prow(own, prow_idx, prow_count):
    count = own.shape[0]
    if prow_count == 4 and count % 32 == 0:
        half = count // 2
        from_x = swap(own, "prow", 1)
        from_y = swap(own, "prow", 2)
        diag_a = swap(from_y[:half], "prow", 1)
        diag_b = swap(from_x[half:], "prow", 2)
        diag = jnp.concatenate([diag_a, diag_b], axis=0)
        return [[(own, prow_idx * count)], [(from_y, jnp.bitwise_xor(prow_idx, 2) * count)],
                [(from_x, jnp.bitwise_xor(prow_idx, 1) * count)], [(diag, jnp.bitwise_xor(prow_idx, 3) * count)]]
    groups = [[(own, prow_idx * count)]]
    for s in range(1, prow_count):
        groups.append([(swap(own, "prow", s), jnp.bitwise_xor(prow_idx, s) * count)])
    return groups


def contract(amplitudes, groups, first, rows, labels, irrep_cols):
    band = lax.dynamic_slice_in_dim(amplitudes, first, rows, axis=0)
    terms = None
    for group in groups:
        for b, o in group:
            window = lax.dynamic_slice_in_dim(band, o, b.shape[0], axis=1)
            same = lax.dynamic_slice_in_dim(labels, o, b.shape[0])[:, None] == irrep_cols[None, :]
            blocked = jnp.where(same, b, jnp.zeros_like(b))
            product = jnp.dot(window, blocked, preferred_element_type=jnp.float32)
            terms = product if terms is None else terms + product
    return terms


def shards(amplitudes, integrals, irrep_rows, irrep_cols, mirror_row):
    prow_count = lax.axis_size("prow")
    cuts_count = lax.axis_size("cuts")
    prow_idx = lax.axis_index("prow")
    cuts_idx = lax.axis_index("cuts")
    width = amplitudes.shape[1]
    labels = lax.dynamic_slice_in_dim(irrep_rows, cuts_idx * width, width)
    groups = gather_prow(integrals, prow_idx, prow_count)
    block_rows = amplitudes.shape[0] // cuts_count
    sent = []
    for s in range(1, cuts_count):
        other = jnp.bitwise_xor(cuts_idx, s)
        sent.append((s, contract(amplitudes, groups, other * block_rows, block_rows, labels, irrep_cols)))
    kept = contract(amplitudes, groups, cuts_idx * block_rows, block_rows, labels, irrep_cols)
    pieces = 2 if block_rows % 16 == 0 else 1
    step = block_rows // pieces
    half = prow_count // 2
    fetched = []
    cycle = []
    for h in range(pieces):
        total = kept[h * step:(h + 1) * step]
        for s, part in sent:
            total = total + swap(part[h * step:(h + 1) * step], "cuts", s)
        cycle.append(total)
        fetched.append(swap(total, "prow", half))
    cycle = jnp.concatenate(cycle, axis=0) if pieces > 1 else cycle[0]
    fetched = jnp.concatenate(fetched, axis=0) if pieces > 1 else fetched[0]
    own_block = prow_idx * cuts_count + cuts_idx
    partner_block = jnp.bitwise_xor(prow_idx, half) * cuts_count + cuts_idx
    mine = lax.dynamic_slice(mirror_row, (own_block * block_rows,), (block_rows,))
    local = mine - partner_block * block_rows
    return cycle - fetched.at[local].get(mode="promise_in_bounds")


def solution(mesh):
    placed = (P("prow", "cuts"), P(("cuts", "prow"), "pcol"), P(), P("pcol"), P())
    return jax.shard_map(
        shards, mesh=mesh, in_specs=placed, out_specs=P(("prow", "cuts"), "pcol"), check_vma=False
    )
```

```python
import jax
import jax.numpy as jnp
from jax import lax
from jax.experimental import pallas as pl
from jax.experimental.pallas import tpu as pltpu
from jax.sharding import PartitionSpec as P


def swap(value, axis, mask):
    return lax.ppermute(value, axis, [(i, i ^ mask) for i in range(lax.axis_size(axis))])


def gather_prow(own, prow_idx, prow_count):
    count = own.shape[0]
    if prow_count == 4 and count % 32 == 0:
        half = count // 2
        from_x = swap(own, "prow", 1)
        from_y = swap(own, "prow", 2)
        diag_a = swap(from_y[:half], "prow", 1)
        diag_b = swap(from_x[half:], "prow", 2)
        base = jnp.bitwise_xor(prow_idx, 3) * count
        return [[(own, prow_idx * count)], [(from_y, jnp.bitwise_xor(prow_idx, 2) * count)],
                [(from_x, jnp.bitwise_xor(prow_idx, 1) * count)], [(diag_a, base), (diag_b, base + half)]]
    groups = [[(own, prow_idx * count)]]
    for s in range(1, prow_count):
        groups.append([(swap(own, "prow", s), jnp.bitwise_xor(prow_idx, s) * count)])
    return groups


def contract(amplitudes, groups, firsts, rows, labels, irrep_cols):
    bands = [lax.dynamic_slice_in_dim(amplitudes, first, rows, axis=0) for first in firsts]
    terms = [None] * len(bands)
    for g, group in enumerate(groups):
        if g == len(groups) - 1 and g > 0:
            blocks, held = lax.optimization_barrier((tuple(b for b, _ in group), tuple(terms)))
            group = [(b, o) for b, (_, o) in zip(blocks, group)]
            terms = list(held)
        for i, band in enumerate(bands):
            for b, o in group:
                window = lax.dynamic_slice_in_dim(band, o, b.shape[0], axis=1)
                same = lax.dynamic_slice_in_dim(labels, o, b.shape[0])[:, None] == irrep_cols[None, :]
                blocked = jnp.where(same, b, jnp.zeros_like(b))
                product = jnp.dot(window, blocked, preferred_element_type=jnp.float32)
                terms[i] = product if terms[i] is None else terms[i] + product
    return terms


def shards(amplitudes, integrals, irrep_rows, irrep_cols, mirror_row):
    prow_count = lax.axis_size("prow")
    cuts_count = lax.axis_size("cuts")
    prow_idx = lax.axis_index("prow")
    cuts_idx = lax.axis_index("cuts")
    width = amplitudes.shape[1]
    labels = lax.dynamic_slice_in_dim(irrep_rows, cuts_idx * width, width)
    groups = gather_prow(integrals, prow_idx, prow_count)
    block_rows = amplitudes.shape[0] // cuts_count
    others = list(range(1, cuts_count))
    firsts = [jnp.bitwise_xor(cuts_idx, s) * block_rows for s in others] + [cuts_idx * block_rows]
    terms = contract(amplitudes, groups, firsts, block_rows, labels, irrep_cols)
    sent = list(zip(others, terms[:-1]))
    kept = terms[-1]
    pieces = 2 if block_rows % 16 == 0 else 1
    step = block_rows // pieces
    half = prow_count // 2
    fetched = []
    cycle = []
    for h in range(pieces):
        total = kept[h * step:(h + 1) * step]
        for s, part in sent:
            total = total + swap(part[h * step:(h + 1) * step], "cuts", s)
        cycle.append(total)
        fetched.append(swap(total, "prow", half))
    cycle = jnp.concatenate(cycle, axis=0) if pieces > 1 else cycle[0]
    fetched = jnp.concatenate(fetched, axis=0) if pieces > 1 else fetched[0]
    own_block = prow_idx * cuts_count + cuts_idx
    partner_block = jnp.bitwise_xor(prow_idx, half) * cuts_count + cuts_idx
    mine = lax.dynamic_slice(mirror_row, (own_block * block_rows,), (block_rows,))
    local = mine - partner_block * block_rows
    return cycle - jnp.take(fetched, local, axis=0, mode="clip")


def solution(mesh):
    placed = (P("prow", "cuts"), P(("cuts", "prow"), "pcol"), P(), P("pcol"), P())
    return jax.shard_map(
        shards, mesh=mesh, in_specs=placed, out_specs=P(("prow", "cuts"), "pcol"), check_vma=False
    )
```

```python
import jax
import jax.numpy as jnp
from jax import lax
from jax.experimental import pallas as pl
from jax.experimental.pallas import tpu as pltpu
from jax.sharding import PartitionSpec as P


def swap(value, axis, mask):
    return lax.ppermute(value, axis, [(i, i ^ mask) for i in range(lax.axis_size(axis))])


def gather_prow(own, prow_idx, prow_count):
    count = own.shape[0]
    if prow_count == 4 and count % 32 == 0:
        half = count // 2
        from_x = swap(own, "prow", 1)
        from_y = swap(own, "prow", 2)
        diag_a = swap(from_y[:half], "prow", 1)
        diag_b = swap(from_x[half:], "prow", 2)
        base = jnp.bitwise_xor(prow_idx, 3) * count
        return [[(own, prow_idx * count)], [(from_y, jnp.bitwise_xor(prow_idx, 2) * count)],
                [(from_x, jnp.bitwise_xor(prow_idx, 1) * count)], [(diag_a, base), (diag_b, base + half)]]
    groups = [[(own, prow_idx * count)]]
    for s in range(1, prow_count):
        groups.append([(swap(own, "prow", s), jnp.bitwise_xor(prow_idx, s) * count)])
    return groups


def contract(amplitudes, groups, firsts, rows, labels, irrep_cols):
    bands = [lax.dynamic_slice_in_dim(amplitudes, first, rows, axis=0) for first in firsts]
    terms = [None] * len(bands)
    for g, group in enumerate(groups):
        if g == len(groups) - 1 and g > 0:
            blocks, held = lax.optimization_barrier((tuple(b for b, _ in group), tuple(terms)))
            group = [(b, o) for b, (_, o) in zip(blocks, group)]
            terms = list(held)
        for i, band in enumerate(bands):
            for b, o in group:
                window = lax.dynamic_slice_in_dim(band, o, b.shape[0], axis=1)
                same = lax.dynamic_slice_in_dim(labels, o, b.shape[0])[:, None] == irrep_cols[None, :]
                blocked = jnp.where(same, b, jnp.zeros_like(b))
                product = jnp.dot(window, blocked, preferred_element_type=jnp.float32)
                terms[i] = product if terms[i] is None else terms[i] + product
    return terms


def shards(amplitudes, integrals, irrep_rows, irrep_cols, mirror_row):
    prow_count = lax.axis_size("prow")
    cuts_count = lax.axis_size("cuts")
    prow_idx = lax.axis_index("prow")
    cuts_idx = lax.axis_index("cuts")
    width = amplitudes.shape[1]
    labels = lax.dynamic_slice_in_dim(irrep_rows, cuts_idx * width, width)
    groups = gather_prow(integrals, prow_idx, prow_count)
    block_rows = amplitudes.shape[0] // cuts_count
    others = list(range(1, cuts_count))
    firsts = [jnp.bitwise_xor(cuts_idx, s) * block_rows for s in others] + [cuts_idx * block_rows]
    terms = contract(amplitudes, groups, firsts, block_rows, labels, irrep_cols)
    sent = list(zip(others, terms[:-1]))
    kept = terms[-1]
    pieces = 1
    step = block_rows // pieces
    half = prow_count // 2
    fetched = []
    cycle = []
    for h in range(pieces):
        total = kept[h * step:(h + 1) * step]
        for s, part in sent:
            total = total + swap(part[h * step:(h + 1) * step], "cuts", s)
        cycle.append(total)
        fetched.append(swap(total, "prow", half))
    cycle = jnp.concatenate(cycle, axis=0) if pieces > 1 else cycle[0]
    fetched = jnp.concatenate(fetched, axis=0) if pieces > 1 else fetched[0]
    own_block = prow_idx * cuts_count + cuts_idx
    partner_block = jnp.bitwise_xor(prow_idx, half) * cuts_count + cuts_idx
    mine = lax.dynamic_slice(mirror_row, (own_block * block_rows,), (block_rows,))
    local = mine - partner_block * block_rows
    return cycle - jnp.take(fetched, local, axis=0, mode="clip")


def solution(mesh):
    placed = (P("prow", "cuts"), P(("cuts", "prow"), "pcol"), P(), P("pcol"), P())
    return jax.shard_map(
        shards, mesh=mesh, in_specs=placed, out_specs=P(("prow", "cuts"), "pcol"), check_vma=False
    )
```

```python
import jax
import jax.numpy as jnp
from jax import lax
from jax.experimental import pallas as pl
from jax.experimental.pallas import tpu as pltpu
from jax.sharding import PartitionSpec as P


def swap(value, axis, mask):
    return lax.ppermute(value, axis, [(i, i ^ mask) for i in range(lax.axis_size(axis))])


def gather_prow(own, prow_idx, prow_count):
    count = own.shape[0]
    if prow_count == 4 and count % 32 == 0:
        h = count // 2
        q = count // 4
        sends = [(swap(own[:h], "prow", 1), swap(own[:h], "prow", 2)),
                 (swap(own[h:], "prow", 1), swap(own[h:], "prow", 2))]
        diags = [jnp.concatenate([swap(y[:q], "prow", 1), swap(x[q:], "prow", 2)], axis=0) for x, y in sends]
        base = [jnp.bitwise_xor(prow_idx, m) * count for m in range(4)]
        return [[(own, base[0])],
                [(sends[0][0], base[1]), (sends[0][1], base[2])],
                [(sends[1][0], base[1] + h), (sends[1][1], base[2] + h)],
                [(diags[0], base[3])],
                [(diags[1], base[3] + h)]]
    if prow_count == 4 and count % 32 == 0:
        half = count // 2
        from_x = swap(own, "prow", 1)
        from_y = swap(own, "prow", 2)
        diag_a = swap(from_y[:half], "prow", 1)
        diag_b = swap(from_x[half:], "prow", 2)
        base = jnp.bitwise_xor(prow_idx, 3) * count
        return [[(own, prow_idx * count)], [(from_y, jnp.bitwise_xor(prow_idx, 2) * count)],
                [(from_x, jnp.bitwise_xor(prow_idx, 1) * count)], [(diag_a, base), (diag_b, base + half)]]
    groups = [[(own, prow_idx * count)]]
    for s in range(1, prow_count):
        groups.append([(swap(own, "prow", s), jnp.bitwise_xor(prow_idx, s) * count)])
    return groups


def contract(amplitudes, groups, firsts, rows, labels, irrep_cols):
    bands = [lax.dynamic_slice_in_dim(amplitudes, first, rows, axis=0) for first in firsts]
    terms = [None] * len(bands)
    for g, group in enumerate(groups):
        if g == len(groups) - 1 and g > 0:
            blocks, held = lax.optimization_barrier((tuple(b for b, _ in group), tuple(terms)))
            group = [(b, o) for b, (_, o) in zip(blocks, group)]
            terms = list(held)
        for i, band in enumerate(bands):
            for b, o in group:
                window = lax.dynamic_slice_in_dim(band, o, b.shape[0], axis=1)
                same = lax.dynamic_slice_in_dim(labels, o, b.shape[0])[:, None] == irrep_cols[None, :]
                blocked = jnp.where(same, b, jnp.zeros_like(b))
                product = jnp.dot(window, blocked, preferred_element_type=jnp.float32)
                terms[i] = product if terms[i] is None else terms[i] + product
    return terms


def shards(amplitudes, integrals, irrep_rows, irrep_cols, mirror_row):
    prow_count = lax.axis_size("prow")
    cuts_count = lax.axis_size("cuts")
    prow_idx = lax.axis_index("prow")
    cuts_idx = lax.axis_index("cuts")
    width = amplitudes.shape[1]
    labels = lax.dynamic_slice_in_dim(irrep_rows, cuts_idx * width, width)
    groups = gather_prow(integrals, prow_idx, prow_count)
    block_rows = amplitudes.shape[0] // cuts_count
    others = list(range(1, cuts_count))
    firsts = [jnp.bitwise_xor(cuts_idx, s) * block_rows for s in others] + [cuts_idx * block_rows]
    terms = contract(amplitudes, groups, firsts, block_rows, labels, irrep_cols)
    sent = list(zip(others, terms[:-1]))
    kept = terms[-1]
    pieces = 1
    step = block_rows // pieces
    half = prow_count // 2
    fetched = []
    cycle = []
    for h in range(pieces):
        total = kept[h * step:(h + 1) * step]
        for s, part in sent:
            total = total + swap(part[h * step:(h + 1) * step], "cuts", s)
        cycle.append(total)
        fetched.append(swap(total, "prow", half))
    cycle = jnp.concatenate(cycle, axis=0) if pieces > 1 else cycle[0]
    fetched = jnp.concatenate(fetched, axis=0) if pieces > 1 else fetched[0]
    own_block = prow_idx * cuts_count + cuts_idx
    partner_block = jnp.bitwise_xor(prow_idx, half) * cuts_count + cuts_idx
    mine = lax.dynamic_slice(mirror_row, (own_block * block_rows,), (block_rows,))
    local = mine - partner_block * block_rows
    return cycle - jnp.take(fetched, local, axis=0, mode="clip")


def solution(mesh):
    placed = (P("prow", "cuts"), P(("cuts", "prow"), "pcol"), P(), P("pcol"), P())
    return jax.shard_map(
        shards, mesh=mesh, in_specs=placed, out_specs=P(("prow", "cuts"), "pcol"), check_vma=False
    )
```

```python
import jax
import jax.numpy as jnp
from jax import lax
from jax.experimental import pallas as pl
from jax.experimental.pallas import tpu as pltpu
from jax.sharding import PartitionSpec as P


def swap(value, axis, mask):
    return lax.ppermute(value, axis, [(i, i ^ mask) for i in range(lax.axis_size(axis))])


def gather_prow(own, prow_idx, prow_count):
    count = own.shape[0]
    if prow_count == 4 and count % 32 == 0:
        half = count // 2
        from_x = swap(own, "prow", 1)
        from_y = swap(own, "prow", 2)
        diag_a = swap(from_y[:half], "prow", 1)
        diag_b = swap(from_x[half:], "prow", 2)
        base = jnp.bitwise_xor(prow_idx, 3) * count
        return [[(own, prow_idx * count)], [(from_y, jnp.bitwise_xor(prow_idx, 2) * count)],
                [(from_x, jnp.bitwise_xor(prow_idx, 1) * count)], [(diag_a, base), (diag_b, base + half)]]
    groups = [[(own, prow_idx * count)]]
    for s in range(1, prow_count):
        groups.append([(swap(own, "prow", s), jnp.bitwise_xor(prow_idx, s) * count)])
    return groups


def contract(amplitudes, groups, firsts, rows, labels, irrep_cols):
    bands = [lax.dynamic_slice_in_dim(amplitudes, first, rows, axis=0) for first in firsts]
    terms = [None] * len(bands)
    for g, group in enumerate(groups):
        if g == len(groups) - 1 and g > 0:
            blocks, held = lax.optimization_barrier((tuple(b for b, _ in group), tuple(terms)))
            group = [(b, o) for b, (_, o) in zip(blocks, group)]
            terms = list(held)
        for i, band in enumerate(bands):
            for b, o in group:
                window = lax.dynamic_slice_in_dim(band, o, b.shape[0], axis=1)
                same = lax.dynamic_slice_in_dim(labels, o, b.shape[0])[:, None] == irrep_cols[None, :]
                blocked = jnp.where(same, b, jnp.zeros_like(b))
                product = jnp.dot(window, blocked, preferred_element_type=jnp.float32)
                terms[i] = product if terms[i] is None else terms[i] + product
    return terms


def shards(amplitudes, integrals, irrep_rows, irrep_cols, mirror_row):
    prow_count = lax.axis_size("prow")
    cuts_count = lax.axis_size("cuts")
    prow_idx = lax.axis_index("prow")
    cuts_idx = lax.axis_index("cuts")
    width = amplitudes.shape[1]
    labels = lax.dynamic_slice_in_dim(irrep_rows, cuts_idx * width, width)
    groups = gather_prow(integrals, prow_idx, prow_count)
    block_rows = amplitudes.shape[0] // cuts_count
    others = list(range(1, cuts_count))
    firsts = [jnp.bitwise_xor(cuts_idx, s) * block_rows for s in others] + [cuts_idx * block_rows]
    terms = contract(amplitudes, groups, firsts, block_rows, labels, irrep_cols)
    sent = list(zip(others, terms[:-1]))
    kept = terms[-1]
    cycle = kept
    for s, part in sent:
        cycle = cycle + swap(part, "cuts", s)
    half = prow_count // 2
    own_block = prow_idx * cuts_count + cuts_idx
    partner_block = jnp.bitwise_xor(prow_idx, half) * cuts_count + cuts_idx
    mine = lax.dynamic_slice(mirror_row, (own_block * block_rows,), (block_rows,))
    local = mine - partner_block * block_rows
    cols = cycle.shape[1]
    pieces = 2 if cols % 16 == 0 else 1
    step = cols // pieces
    results = []
    for j in range(pieces):
        piece = cycle[:, j * step:(j + 1) * step]
        fetched = swap(piece, "prow", half)
        results.append(piece - jnp.take(fetched, local, axis=0, mode="clip"))
    return jnp.concatenate(results, axis=1) if pieces > 1 else results[0]


def solution(mesh):
    placed = (P("prow", "cuts"), P(("cuts", "prow"), "pcol"), P(), P("pcol"), P())
    return jax.shard_map(
        shards, mesh=mesh, in_specs=placed, out_specs=P(("prow", "cuts"), "pcol"), check_vma=False
    )
```

```python
import jax
import jax.numpy as jnp
from jax import lax
from jax.experimental import pallas as pl
from jax.experimental.pallas import tpu as pltpu
from jax.sharding import PartitionSpec as P


def swap(value, axis, mask):
    return lax.ppermute(value, axis, [(i, i ^ mask) for i in range(lax.axis_size(axis))])


def gather_prow(own, prow_idx, prow_count):
    count = own.shape[0]
    if prow_count == 4 and count % 32 == 0:
        half = count // 2
        from_x = swap(own, "prow", 1)
        from_y = swap(own, "prow", 2)
        diag_a = swap(from_y[:half], "prow", 1)
        diag_b = swap(from_x[half:], "prow", 2)
        base = jnp.bitwise_xor(prow_idx, 3) * count
        return [[(own, prow_idx * count)], [(from_y, jnp.bitwise_xor(prow_idx, 2) * count)],
                [(from_x, jnp.bitwise_xor(prow_idx, 1) * count)], [(diag_a, base), (diag_b, base + half)]]
    groups = [[(own, prow_idx * count)]]
    for s in range(1, prow_count):
        groups.append([(swap(own, "prow", s), jnp.bitwise_xor(prow_idx, s) * count)])
    return groups


def contract(amplitudes, groups, firsts, rows, labels, irrep_cols):
    bands = [lax.dynamic_slice_in_dim(amplitudes, first, rows, axis=0) for first in firsts]
    terms = [None] * len(bands)
    for g, group in enumerate(groups):
        if g == len(groups) - 1 and g > 0:
            blocks, held = lax.optimization_barrier((tuple(b for b, _ in group), tuple(terms)))
            group = [(b, o) for b, (_, o) in zip(blocks, group)]
            terms = list(held)
        for i, band in enumerate(bands):
            for b, o in group:
                window = lax.dynamic_slice_in_dim(band, o, b.shape[0], axis=1)
                same = lax.dynamic_slice_in_dim(labels, o, b.shape[0])[:, None] == irrep_cols[None, :]
                blocked = jnp.where(same, b, jnp.zeros_like(b))
                product = jnp.dot(window, blocked, preferred_element_type=jnp.float32)
                terms[i] = product if terms[i] is None else terms[i] + product
    return terms


def shards(amplitudes, integrals, irrep_rows, irrep_cols, mirror_row):
    prow_count = lax.axis_size("prow")
    cuts_count = lax.axis_size("cuts")
    prow_idx = lax.axis_index("prow")
    cuts_idx = lax.axis_index("cuts")
    width = amplitudes.shape[1]
    labels = lax.dynamic_slice_in_dim(irrep_rows, cuts_idx * width, width)
    groups = gather_prow(integrals, prow_idx, prow_count)
    block_rows = amplitudes.shape[0] // cuts_count
    others = list(range(1, cuts_count))
    firsts = [jnp.bitwise_xor(cuts_idx, s) * block_rows for s in others] + [cuts_idx * block_rows]
    terms = contract(amplitudes, groups, firsts, block_rows, labels, irrep_cols)
    sent = list(zip(others, terms[:-1]))
    kept = terms[-1]
    half = prow_count // 2
    own_block = prow_idx * cuts_count + cuts_idx
    partner_block = jnp.bitwise_xor(prow_idx, half) * cuts_count + cuts_idx
    mine = lax.dynamic_slice(mirror_row, (own_block * block_rows,), (block_rows,))
    local = mine - partner_block * block_rows
    cols = kept.shape[1]
    pieces = 2 if cols % 16 == 0 else 1
    step = cols // pieces
    results = []
    for j in range(pieces):
        piece = kept[:, j * step:(j + 1) * step]
        for s, part in sent:
            piece = piece + swap(part[:, j * step:(j + 1) * step], "cuts", s)
        fetched = swap(piece, "prow", half)
        results.append(piece - jnp.take(fetched, local, axis=0, mode="clip"))
    return jnp.concatenate(results, axis=1) if pieces > 1 else results[0]


def solution(mesh):
    placed = (P("prow", "cuts"), P(("cuts", "prow"), "pcol"), P(), P("pcol"), P())
    return jax.shard_map(
        shards, mesh=mesh, in_specs=placed, out_specs=P(("prow", "cuts"), "pcol"), check_vma=False
    )
```

```python
import jax
import jax.numpy as jnp
from jax import lax
from jax.experimental import pallas as pl
from jax.experimental.pallas import tpu as pltpu
from jax.sharding import PartitionSpec as P


def swap(value, axis, mask):
    return lax.ppermute(value, axis, [(i, i ^ mask) for i in range(lax.axis_size(axis))])


def gather_prow(own, prow_idx, prow_count):
    count = own.shape[0]
    if prow_count == 4 and count % 32 == 0:
        half = count // 2
        from_x = swap(own, "prow", 1)
        from_y = swap(own, "prow", 2)
        diag_a = swap(from_y[:half], "prow", 1)
        diag_b = swap(from_x[half:], "prow", 2)
        base = jnp.bitwise_xor(prow_idx, 3) * count
        return [[(own, prow_idx * count)], [(from_y, jnp.bitwise_xor(prow_idx, 2) * count)],
                [(from_x, jnp.bitwise_xor(prow_idx, 1) * count)], [(diag_a, base), (diag_b, base + half)]]
    groups = [[(own, prow_idx * count)]]
    for s in range(1, prow_count):
        groups.append([(swap(own, "prow", s), jnp.bitwise_xor(prow_idx, s) * count)])
    return groups


def contract(amplitudes, groups, firsts, rows, labels, irrep_cols):
    bands = [lax.dynamic_slice_in_dim(amplitudes, first, rows, axis=0) for first in firsts]
    terms = [None] * len(bands)
    for g, group in enumerate(groups):
        if g == len(groups) - 1 and g > 0:
            blocks, held = lax.optimization_barrier((tuple(b for b, _ in group), tuple(terms)))
            group = [(b, o) for b, (_, o) in zip(blocks, group)]
            terms = list(held)
        for i, band in enumerate(bands):
            for b, o in group:
                window = lax.dynamic_slice_in_dim(band, o, b.shape[0], axis=1)
                same = lax.dynamic_slice_in_dim(labels, o, b.shape[0])[:, None] == irrep_cols[None, :]
                blocked = jnp.where(same, b, jnp.zeros_like(b))
                product = jnp.dot(window, blocked, preferred_element_type=jnp.float32)
                terms[i] = product if terms[i] is None else terms[i] + product
    return terms


def shards(amplitudes, integrals, irrep_rows, irrep_cols, mirror_row):
    prow_count = lax.axis_size("prow")
    cuts_count = lax.axis_size("cuts")
    prow_idx = lax.axis_index("prow")
    cuts_idx = lax.axis_index("cuts")
    width = amplitudes.shape[1]
    labels = lax.dynamic_slice_in_dim(irrep_rows, cuts_idx * width, width)
    groups = gather_prow(integrals, prow_idx, prow_count)
    block_rows = amplitudes.shape[0] // cuts_count
    others = list(range(1, cuts_count))
    firsts = [jnp.bitwise_xor(cuts_idx, s) * block_rows for s in others] + [cuts_idx * block_rows]
    terms = contract(amplitudes, groups, firsts, block_rows, labels, irrep_cols)
    sent = list(zip(others, terms[:-1]))
    kept = terms[-1]
    half = prow_count // 2
    own_block = prow_idx * cuts_count + cuts_idx
    partner_block = jnp.bitwise_xor(prow_idx, half) * cuts_count + cuts_idx
    mine = lax.dynamic_slice(mirror_row, (own_block * block_rows,), (block_rows,))
    local = mine - partner_block * block_rows
    theirs = lax.dynamic_slice(mirror_row, (partner_block * block_rows,), (block_rows,))
    wanted = theirs - own_block * block_rows
    cols = kept.shape[1]
    pieces = 2 if cols % 16 == 0 else 1
    step = cols // pieces
    results = []
    for j in range(pieces):
        piece = kept[:, j * step:(j + 1) * step]
        for s, part in sent:
            piece = piece + swap(part[:, j * step:(j + 1) * step], "cuts", s)
        if j == pieces - 1 and pieces > 1:
            fetched = swap(jnp.take(piece, wanted, axis=0, mode="clip"), "prow", half)
            results.append(piece - fetched)
        else:
            fetched = swap(piece, "prow", half)
            results.append(piece - jnp.take(fetched, local, axis=0, mode="clip"))
    return jnp.concatenate(results, axis=1) if pieces > 1 else results[0]


def solution(mesh):
    placed = (P("prow", "cuts"), P(("cuts", "prow"), "pcol"), P(), P("pcol"), P())
    return jax.shard_map(
        shards, mesh=mesh, in_specs=placed, out_specs=P(("prow", "cuts"), "pcol"), check_vma=False
    )
```

```python
import jax
import jax.numpy as jnp
from jax import lax
from jax.experimental import pallas as pl
from jax.experimental.pallas import tpu as pltpu
from jax.sharding import PartitionSpec as P


def swap(value, axis, mask):
    return lax.ppermute(value, axis, [(i, i ^ mask) for i in range(lax.axis_size(axis))])


def gather_prow(own, prow_idx, prow_count):
    count = own.shape[0]
    if prow_count == 4 and count % 32 == 0:
        half = count // 2
        from_x = swap(own, "prow", 1)
        from_y = swap(own, "prow", 2)
        diag_a = swap(from_y[:half], "prow", 1)
        diag_b = swap(from_x[half:], "prow", 2)
        base = jnp.bitwise_xor(prow_idx, 3) * count
        return [[(own, prow_idx * count)], [(from_y, jnp.bitwise_xor(prow_idx, 2) * count)],
                [(from_x, jnp.bitwise_xor(prow_idx, 1) * count)], [(diag_b, base + half)], [(diag_a, base)]]
    groups = [[(own, prow_idx * count)]]
    for s in range(1, prow_count):
        groups.append([(swap(own, "prow", s), jnp.bitwise_xor(prow_idx, s) * count)])
    return groups


def contract(amplitudes, groups, firsts, rows, labels, irrep_cols):
    bands = [lax.dynamic_slice_in_dim(amplitudes, first, rows, axis=0) for first in firsts]
    terms = [None] * len(bands)
    for g, group in enumerate(groups):
        if g == len(groups) - 1 and g > 0:
            blocks, held = lax.optimization_barrier((tuple(b for b, _ in group), tuple(terms)))
            group = [(b, o) for b, (_, o) in zip(blocks, group)]
            terms = list(held)
        for i, band in enumerate(bands):
            for b, o in group:
                window = lax.dynamic_slice_in_dim(band, o, b.shape[0], axis=1)
                same = lax.dynamic_slice_in_dim(labels, o, b.shape[0])[:, None] == irrep_cols[None, :]
                blocked = jnp.where(same, b, jnp.zeros_like(b))
                product = jnp.dot(window, blocked, preferred_element_type=jnp.float32)
                terms[i] = product if terms[i] is None else terms[i] + product
    return terms


def shards(amplitudes, integrals, irrep_rows, irrep_cols, mirror_row):
    prow_count = lax.axis_size("prow")
    cuts_count = lax.axis_size("cuts")
    prow_idx = lax.axis_index("prow")
    cuts_idx = lax.axis_index("cuts")
    width = amplitudes.shape[1]
    labels = lax.dynamic_slice_in_dim(irrep_rows, cuts_idx * width, width)
    groups = gather_prow(integrals, prow_idx, prow_count)
    block_rows = amplitudes.shape[0] // cuts_count
    others = list(range(1, cuts_count))
    firsts = [jnp.bitwise_xor(cuts_idx, s) * block_rows for s in others] + [cuts_idx * block_rows]
    terms = contract(amplitudes, groups, firsts, block_rows, labels, irrep_cols)
    sent = list(zip(others, terms[:-1]))
    kept = terms[-1]
    half = prow_count // 2
    own_block = prow_idx * cuts_count + cuts_idx
    partner_block = jnp.bitwise_xor(prow_idx, half) * cuts_count + cuts_idx
    mine = lax.dynamic_slice(mirror_row, (own_block * block_rows,), (block_rows,))
    local = mine - partner_block * block_rows
    theirs = lax.dynamic_slice(mirror_row, (partner_block * block_rows,), (block_rows,))
    wanted = theirs - own_block * block_rows
    cols = kept.shape[1]
    pieces = 2 if cols % 16 == 0 else 1
    step = cols // pieces
    results = []
    for j in range(pieces):
        piece = kept[:, j * step:(j + 1) * step]
        for s, part in sent:
            piece = piece + swap(part[:, j * step:(j + 1) * step], "cuts", s)
        if j == pieces - 1 and pieces > 1:
            fetched = swap(jnp.take(piece, wanted, axis=0, mode="clip"), "prow", half)
            results.append(piece - fetched)
        else:
            fetched = swap(piece, "prow", half)
            results.append(piece - jnp.take(fetched, local, axis=0, mode="clip"))
    return jnp.concatenate(results, axis=1) if pieces > 1 else results[0]


def solution(mesh):
    placed = (P("prow", "cuts"), P(("cuts", "prow"), "pcol"), P(), P("pcol"), P())
    return jax.shard_map(
        shards, mesh=mesh, in_specs=placed, out_specs=P(("prow", "cuts"), "pcol"), check_vma=False
    )
```

```python
import jax
import jax.numpy as jnp
from jax import lax
from jax.sharding import PartitionSpec as P


def swap(value, axis, mask):
    return lax.ppermute(value, axis, [(i, i ^ mask) for i in range(lax.axis_size(axis))])


def gather_prow(own, prow_idx, prow_count):
    count = own.shape[0]
    if prow_count == 4 and count % 32 == 0:
        half = count // 2
        from_x = swap(own, "prow", 1)
        from_y = swap(own, "prow", 2)
        diag_a = swap(from_y[:half], "prow", 1)
        diag_b = swap(from_x[half:], "prow", 2)
        diag = jnp.concatenate([diag_a, diag_b], axis=0)
        return [[(own, prow_idx * count)], [(from_y, jnp.bitwise_xor(prow_idx, 2) * count)],
                [(from_x, jnp.bitwise_xor(prow_idx, 1) * count)], [(diag, jnp.bitwise_xor(prow_idx, 3) * count)]]
    groups = [[(own, prow_idx * count)]]
    for s in range(1, prow_count):
        groups.append([(swap(own, "prow", s), jnp.bitwise_xor(prow_idx, s) * count)])
    return groups


def contract(amplitudes, groups, firsts, rows, labels, irrep_cols):
    bands = [lax.dynamic_slice_in_dim(amplitudes, first, rows, axis=0) for first in firsts]
    terms = [None] * len(bands)
    for g, group in enumerate(groups):
        if g == len(groups) - 1 and g > 0:
            blocks, held = lax.optimization_barrier((tuple(b for b, _ in group), tuple(terms)))
            group = [(b, o) for b, (_, o) in zip(blocks, group)]
            terms = list(held)
        for i, band in enumerate(bands):
            for b, o in group:
                window = lax.dynamic_slice_in_dim(band, o, b.shape[0], axis=1)
                same = lax.dynamic_slice_in_dim(labels, o, b.shape[0])[:, None] == irrep_cols[None, :]
                blocked = jnp.where(same, b, jnp.zeros_like(b))
                product = jnp.dot(window, blocked, preferred_element_type=jnp.float32)
                terms[i] = product if terms[i] is None else terms[i] + product
    return terms


def shards(amplitudes, integrals, irrep_rows, irrep_cols, mirror_row):
    prow_count = lax.axis_size("prow")
    cuts_count = lax.axis_size("cuts")
    prow_idx = lax.axis_index("prow")
    cuts_idx = lax.axis_index("cuts")
    width = amplitudes.shape[1]
    labels = lax.dynamic_slice_in_dim(irrep_rows, cuts_idx * width, width)
    groups = gather_prow(integrals, prow_idx, prow_count)
    block_rows = amplitudes.shape[0] // cuts_count
    others = list(range(1, cuts_count))
    firsts = [jnp.bitwise_xor(cuts_idx, s) * block_rows for s in others] + [cuts_idx * block_rows]
    terms = contract(amplitudes, groups, firsts, block_rows, labels, irrep_cols)
    sent = list(zip(others, terms[:-1]))
    kept = terms[-1]
    half = prow_count // 2
    own_block = prow_idx * cuts_count + cuts_idx
    partner_block = jnp.bitwise_xor(prow_idx, half) * cuts_count + cuts_idx
    mine = lax.dynamic_slice(mirror_row, (own_block * block_rows,), (block_rows,))
    local = mine - partner_block * block_rows
    theirs = lax.dynamic_slice(mirror_row, (partner_block * block_rows,), (block_rows,))
    wanted = theirs - own_block * block_rows
    cols = kept.shape[1]
    pieces = 2 if cols % 16 == 0 else 1
    step = cols // pieces
    results = []
    for j in range(pieces):
        piece = kept[:, j * step:(j + 1) * step]
        for s, part in sent:
            piece = piece + swap(part[:, j * step:(j + 1) * step], "cuts", s)
        if j == pieces - 1 and pieces > 1:
            fetched = swap(jnp.take(piece, wanted, axis=0, mode="clip"), "prow", half)
            results.append(piece - fetched)
        else:
            fetched = swap(piece, "prow", half)
            results.append(piece - jnp.take(fetched, local, axis=0, mode="clip"))
    return jnp.concatenate(results, axis=1) if pieces > 1 else results[0]


def solution(mesh):
    placed = (P("prow", "cuts"), P(("cuts", "prow"), "pcol"), P(), P("pcol"), P())
    return jax.shard_map(
        shards, mesh=mesh, in_specs=placed, out_specs=P(("prow", "cuts"), "pcol"), check_vma=False
    )
```

```python
import jax
import jax.numpy as jnp
from jax import lax
from jax.experimental import pallas as pl
from jax.experimental.pallas import tpu as pltpu
from jax.sharding import PartitionSpec as P


def swap(value, axis, mask):
    return lax.ppermute(value, axis, [(i, i ^ mask) for i in range(lax.axis_size(axis))])


def gather_prow(own, prow_idx, prow_count, pieces):
    count, cols = own.shape
    step = cols // pieces
    if prow_count == 4 and count % 32 == 0 and pieces == 2:
        half = count // 2
        from_x = swap(own, "prow", 1)
        from_y = swap(own, "prow", 2)
        diag_a = swap(from_y[:half, :step], "prow", 1)
        diag_b = swap(from_x[half:, :step], "prow", 2)
        rest, _ = lax.optimization_barrier((from_y[:, step:], diag_a))
        diag_c = swap(rest, "prow", 1)
        base = jnp.bitwise_xor(prow_idx, 3) * count
        return [[(own, prow_idx * count, 0)], [(from_y, jnp.bitwise_xor(prow_idx, 2) * count, 0)],
                [(from_x, jnp.bitwise_xor(prow_idx, 1) * count, 0)],
                [(diag_a, base, 0), (diag_b, base + half, 0)], [(diag_c, base, step)]]
    groups = [[(own, prow_idx * count, 0)]]
    for s in range(1, prow_count):
        groups.append([(swap(own, "prow", s), jnp.bitwise_xor(prow_idx, s) * count, 0)])
    return groups


def contract(amplitudes, groups, firsts, rows, labels, irrep_cols, pieces):
    bands = [lax.dynamic_slice_in_dim(amplitudes, first, rows, axis=0) for first in firsts]
    cols = irrep_cols.shape[0]
    step = cols // pieces
    full = [None] * len(bands)
    parts = [None] * len(bands)
    split = [g for g, group in enumerate(groups) if any(b.shape[1] != cols for b, _, _ in group)]
    held_at = split[0] if split else len(groups) - 1
    for g, group in enumerate(groups):
        if g == held_at and g > 0:
            blocks, held = lax.optimization_barrier((tuple(b for b, _, _ in group), (tuple(full), tuple(parts))))
            group = [(b, o, c) for b, (_, o, c) in zip(blocks, group)]
            full, parts = list(held[0]), list(held[1])
        for i, band in enumerate(bands):
            for b, o, c in group:
                w = b.shape[1]
                window = lax.dynamic_slice_in_dim(band, o, b.shape[0], axis=1)
                same = lax.dynamic_slice_in_dim(labels, o, b.shape[0])[:, None] == irrep_cols[None, c:c + w]
                blocked = jnp.where(same, b, jnp.zeros_like(b))
                product = jnp.dot(window, blocked, preferred_element_type=jnp.float32)
                if w != cols and parts[i] is None:
                    parts[i] = tuple(full[i][:, j * step:(j + 1) * step] for j in range(pieces))
                    full[i] = None
                if parts[i] is None:
                    full[i] = product if full[i] is None else full[i] + product
                elif w == cols:
                    parts[i] = tuple(p + product[:, j * step:(j + 1) * step] for j, p in enumerate(parts[i]))
                else:
                    j = c // step
                    parts[i] = parts[i][:j] + (parts[i][j] + product,) + parts[i][j + 1:]
    return [p if p is not None else tuple(t[:, j * step:(j + 1) * step] for j in range(pieces))
            for p, t in zip(parts, full)]


def shards(amplitudes, integrals, irrep_rows, irrep_cols, mirror_row):
    prow_count = lax.axis_size("prow")
    cuts_count = lax.axis_size("cuts")
    prow_idx = lax.axis_index("prow")
    cuts_idx = lax.axis_index("cuts")
    width = amplitudes.shape[1]
    cols = integrals.shape[1]
    pieces = 2 if cols % 16 == 0 else 1
    labels = lax.dynamic_slice_in_dim(irrep_rows, cuts_idx * width, width)
    groups = gather_prow(integrals, prow_idx, prow_count, pieces)
    block_rows = amplitudes.shape[0] // cuts_count
    others = list(range(1, cuts_count))
    firsts = [jnp.bitwise_xor(cuts_idx, s) * block_rows for s in others] + [cuts_idx * block_rows]
    late = groups[-1] if pieces > 1 and all(c == cols - cols // pieces for _, _, c in groups[-1]) else None
    if late is not None:
        groups = groups[:-1]
    terms = contract(amplitudes, groups, firsts, block_rows, labels, irrep_cols, pieces)
    terms = [list(t) for t in terms]
    half = prow_count // 2
    own_block = prow_idx * cuts_count + cuts_idx
    partner_block = jnp.bitwise_xor(prow_idx, half) * cuts_count + cuts_idx
    mine = lax.dynamic_slice(mirror_row, (own_block * block_rows,), (block_rows,))
    local = mine - partner_block * block_rows
    theirs = lax.dynamic_slice(mirror_row, (partner_block * block_rows,), (block_rows,))
    wanted = theirs - own_block * block_rows
    results = []
    previous = None
    for j in range(pieces):
        if late is not None and j == pieces - 1:
            blocks, _ = lax.optimization_barrier((tuple(b for b, _, _ in late), previous))
            for i, first in enumerate(firsts):
                band = lax.dynamic_slice_in_dim(amplitudes, first, block_rows, axis=0)
                for b, (_, o, c) in zip(blocks, late):
                    window = lax.dynamic_slice_in_dim(band, o, b.shape[0], axis=1)
                    same = lax.dynamic_slice_in_dim(labels, o, b.shape[0])[:, None] == irrep_cols[None, c:]
                    blocked = jnp.where(same, b, jnp.zeros_like(b))
                    terms[i][j] = terms[i][j] + jnp.dot(window, blocked, preferred_element_type=jnp.float32)
        piece = terms[-1][j]
        for s, part in zip(others, terms[:-1]):
            piece = piece + swap(part[j], "cuts", s)
        previous = piece
        if j == pieces - 1 and pieces > 1:
            fetched = swap(jnp.take(piece, wanted, axis=0, mode="clip"), "prow", half)
            results.append(piece - fetched)
        else:
            fetched = swap(piece, "prow", half)
            results.append(piece - jnp.take(fetched, local, axis=0, mode="clip"))
    return jnp.concatenate(results, axis=1) if pieces > 1 else results[0]


def solution(mesh):
    placed = (P("prow", "cuts"), P(("cuts", "prow"), "pcol"), P(), P("pcol"), P())
    return jax.shard_map(
        shards, mesh=mesh, in_specs=placed, out_specs=P(("prow", "cuts"), "pcol"), check_vma=False
    )
```

```python
import jax
import jax.numpy as jnp
from jax import lax
from jax.experimental import pallas as pl
from jax.experimental.pallas import tpu as pltpu
from jax.sharding import PartitionSpec as P


def swap(value, axis, mask):
    return lax.ppermute(value, axis, [(i, i ^ mask) for i in range(lax.axis_size(axis))])


def gather_prow(own, prow_idx, prow_count):
    count = own.shape[0]
    if prow_count == 4 and count % 32 == 0:
        half = count // 2
        from_x = swap(own, "prow", 1)
        from_y = swap(own, "prow", 2)
        diag_a = swap(from_y[:half], "prow", 1)
        diag_b = swap(from_x[half:], "prow", 2)
        base = jnp.bitwise_xor(prow_idx, 3) * count
        return [[(own, prow_idx * count)], [(from_y, jnp.bitwise_xor(prow_idx, 2) * count)],
                [(from_x, jnp.bitwise_xor(prow_idx, 1) * count)], [(diag_a, base), (diag_b, base + half)]]
    groups = [[(own, prow_idx * count)]]
    for s in range(1, prow_count):
        groups.append([(swap(own, "prow", s), jnp.bitwise_xor(prow_idx, s) * count)])
    return groups


def contract(amplitudes, groups, firsts, rows, labels, irrep_cols):
    bands = [lax.dynamic_slice_in_dim(amplitudes, first, rows, axis=0) for first in firsts]
    terms = [None] * len(bands)
    for g, group in enumerate(groups):
        if g == len(groups) - 1 and g > 0:
            blocks, held = lax.optimization_barrier((tuple(b for b, _ in group), tuple(terms)))
            group = [(b, o) for b, (_, o) in zip(blocks, group)]
            terms = list(held)
        for i, band in enumerate(bands):
            for b, o in group:
                window = lax.dynamic_slice_in_dim(band, o, b.shape[0], axis=1)
                same = lax.dynamic_slice_in_dim(labels, o, b.shape[0])[:, None] == irrep_cols[None, :]
                blocked = jnp.where(same, b, jnp.zeros_like(b))
                product = jnp.dot(window, blocked, preferred_element_type=jnp.float32)
                terms[i] = product if terms[i] is None else terms[i] + product
    return terms


def shards(amplitudes, integrals, irrep_rows, irrep_cols, mirror_row):
    prow_count = lax.axis_size("prow")
    cuts_count = lax.axis_size("cuts")
    prow_idx = lax.axis_index("prow")
    cuts_idx = lax.axis_index("cuts")
    width = amplitudes.shape[1]
    labels = lax.dynamic_slice_in_dim(irrep_rows, cuts_idx * width, width)
    groups = gather_prow(integrals, prow_idx, prow_count)
    block_rows = amplitudes.shape[0] // cuts_count
    others = list(range(1, cuts_count))
    firsts = [jnp.bitwise_xor(cuts_idx, s) * block_rows for s in others] + [cuts_idx * block_rows]
    terms = contract(amplitudes, groups, firsts, block_rows, labels, irrep_cols)
    sent = list(zip(others, terms[:-1]))
    kept = terms[-1]
    half = prow_count // 2
    own_block = prow_idx * cuts_count + cuts_idx
    partner_block = jnp.bitwise_xor(prow_idx, half) * cuts_count + cuts_idx
    mine = lax.dynamic_slice(mirror_row, (own_block * block_rows,), (block_rows,))
    local = mine - partner_block * block_rows
    theirs = lax.dynamic_slice(mirror_row, (partner_block * block_rows,), (block_rows,))
    wanted = theirs - own_block * block_rows
    cols = kept.shape[1]
    pieces = 4 if cols % 4 == 0 else 1
    step = cols // pieces
    results = []
    for j in range(pieces):
        piece = kept[:, j * step:(j + 1) * step]
        for s, part in sent:
            piece = piece + swap(part[:, j * step:(j + 1) * step], "cuts", s)
        if j == pieces - 1 and pieces > 1:
            fetched = swap(jnp.take(piece, wanted, axis=0, mode="clip"), "prow", half)
            results.append(piece - fetched)
        else:
            fetched = swap(piece, "prow", half)
            results.append(piece - jnp.take(fetched, local, axis=0, mode="clip"))
    return jnp.concatenate(results, axis=1) if pieces > 1 else results[0]


def solution(mesh):
    placed = (P("prow", "cuts"), P(("cuts", "prow"), "pcol"), P(), P("pcol"), P())
    return jax.shard_map(
        shards, mesh=mesh, in_specs=placed, out_specs=P(("prow", "cuts"), "pcol"), check_vma=False
    )
```

```python
import jax
import jax.numpy as jnp
from jax import lax
from jax.experimental import pallas as pl
from jax.experimental.pallas import tpu as pltpu
from jax.sharding import PartitionSpec as P


def swap(value, axis, mask):
    return lax.ppermute(value, axis, [(i, i ^ mask) for i in range(lax.axis_size(axis))])


def gather_prow(own, prow_idx, prow_count):
    count = own.shape[0]
    if prow_count == 4 and count % 32 == 0:
        half = count // 2
        from_x = swap(own, "prow", 1)
        from_y = swap(own, "prow", 2)
        diag_a = swap(from_y[:half], "prow", 1)
        diag_b = swap(from_x[half:], "prow", 2)
        base = jnp.bitwise_xor(prow_idx, 3) * count
        return [[(own, prow_idx * count)], [(from_y, jnp.bitwise_xor(prow_idx, 2) * count)],
                [(from_x, jnp.bitwise_xor(prow_idx, 1) * count)], [(diag_a, base), (diag_b, base + half)]]
    groups = [[(own, prow_idx * count)]]
    for s in range(1, prow_count):
        groups.append([(swap(own, "prow", s), jnp.bitwise_xor(prow_idx, s) * count)])
    return groups


def contract(amplitudes, groups, firsts, rows, labels, irrep_cols):
    bands = [lax.dynamic_slice_in_dim(amplitudes, first, rows, axis=0) for first in firsts]
    terms = [None] * len(bands)
    for g, group in enumerate(groups):
        if g == len(groups) - 1 and g > 0:
            blocks, held = lax.optimization_barrier((tuple(b for b, _ in group), tuple(terms)))
            group = [(b, o) for b, (_, o) in zip(blocks, group)]
            terms = list(held)
        for i, band in enumerate(bands):
            for b, o in group:
                window = lax.dynamic_slice_in_dim(band, o, b.shape[0], axis=1)
                same = lax.dynamic_slice_in_dim(labels, o, b.shape[0])[:, None] == irrep_cols[None, :]
                blocked = jnp.where(same, b, jnp.zeros_like(b))
                product = jnp.dot(window, blocked, preferred_element_type=jnp.float32)
                terms[i] = product if terms[i] is None else terms[i] + product
    return terms


def shards(amplitudes, integrals, irrep_rows, irrep_cols, mirror_row):
    prow_count = lax.axis_size("prow")
    cuts_count = lax.axis_size("cuts")
    prow_idx = lax.axis_index("prow")
    cuts_idx = lax.axis_index("cuts")
    width = amplitudes.shape[1]
    labels = lax.dynamic_slice_in_dim(irrep_rows, cuts_idx * width, width)
    groups = gather_prow(integrals, prow_idx, prow_count)
    block_rows = amplitudes.shape[0] // cuts_count
    others = list(range(1, cuts_count))
    firsts = [jnp.bitwise_xor(cuts_idx, s) * block_rows for s in others] + [cuts_idx * block_rows]
    terms = contract(amplitudes, groups, firsts, block_rows, labels, irrep_cols)
    sent = list(zip(others, terms[:-1]))
    kept = terms[-1]
    half = prow_count // 2
    own_block = prow_idx * cuts_count + cuts_idx
    partner_block = jnp.bitwise_xor(prow_idx, half) * cuts_count + cuts_idx
    mine = lax.dynamic_slice(mirror_row, (own_block * block_rows,), (block_rows,))
    local = mine - partner_block * block_rows
    theirs = lax.dynamic_slice(mirror_row, (partner_block * block_rows,), (block_rows,))
    wanted = theirs - own_block * block_rows
    cols = kept.shape[1]
    first = cols // 3 // 16 * 16
    bounds = [0, first, cols] if first > 0 else [0, cols]
    pieces = len(bounds) - 1
    results = []
    for j in range(pieces):
        lo, hi = bounds[j], bounds[j + 1]
        piece = kept[:, lo:hi]
        for s, part in sent:
            piece = piece + swap(part[:, lo:hi], "cuts", s)
        if j == pieces - 1 and pieces > 1:
            fetched = swap(jnp.take(piece, wanted, axis=0, mode="clip"), "prow", half)
            results.append(piece - fetched)
        else:
            fetched = swap(piece, "prow", half)
            results.append(piece - jnp.take(fetched, local, axis=0, mode="clip"))
    return jnp.concatenate(results, axis=1) if pieces > 1 else results[0]


def solution(mesh):
    placed = (P("prow", "cuts"), P(("cuts", "prow"), "pcol"), P(), P("pcol"), P())
    return jax.shard_map(
        shards, mesh=mesh, in_specs=placed, out_specs=P(("prow", "cuts"), "pcol"), check_vma=False
    )
```

```python
import jax
import jax.numpy as jnp
from jax import lax
from jax.experimental import pallas as pl
from jax.experimental.pallas import tpu as pltpu
from jax.sharding import PartitionSpec as P


def swap(value, axis, mask):
    return lax.ppermute(value, axis, [(i, i ^ mask) for i in range(lax.axis_size(axis))])


def gather_prow(own, prow_idx, prow_count):
    count = own.shape[0]
    if prow_count == 4 and count % 32 == 0:
        half = count // 2 + count // 16 // 16 * 16
        from_x = swap(own, "prow", 1)
        from_y = swap(own, "prow", 2)
        diag_a = swap(from_y[:half], "prow", 1)
        diag_b = swap(from_x[half:], "prow", 2)
        base = jnp.bitwise_xor(prow_idx, 3) * count
        return [[(own, prow_idx * count)], [(from_y, jnp.bitwise_xor(prow_idx, 2) * count)],
                [(from_x, jnp.bitwise_xor(prow_idx, 1) * count)], [(diag_a, base), (diag_b, base + half)]]
    groups = [[(own, prow_idx * count)]]
    for s in range(1, prow_count):
        groups.append([(swap(own, "prow", s), jnp.bitwise_xor(prow_idx, s) * count)])
    return groups


def contract(amplitudes, groups, firsts, rows, labels, irrep_cols):
    bands = [lax.dynamic_slice_in_dim(amplitudes, first, rows, axis=0) for first in firsts]
    terms = [None] * len(bands)
    for g, group in enumerate(groups):
        if g == len(groups) - 1 and g > 0:
            blocks, held = lax.optimization_barrier((tuple(b for b, _ in group), tuple(terms)))
            group = [(b, o) for b, (_, o) in zip(blocks, group)]
            terms = list(held)
        for i, band in enumerate(bands):
            for b, o in group:
                window = lax.dynamic_slice_in_dim(band, o, b.shape[0], axis=1)
                same = lax.dynamic_slice_in_dim(labels, o, b.shape[0])[:, None] == irrep_cols[None, :]
                blocked = jnp.where(same, b, jnp.zeros_like(b))
                product = jnp.dot(window, blocked, preferred_element_type=jnp.float32)
                terms[i] = product if terms[i] is None else terms[i] + product
    return terms


def shards(amplitudes, integrals, irrep_rows, irrep_cols, mirror_row):
    prow_count = lax.axis_size("prow")
    cuts_count = lax.axis_size("cuts")
    prow_idx = lax.axis_index("prow")
    cuts_idx = lax.axis_index("cuts")
    width = amplitudes.shape[1]
    labels = lax.dynamic_slice_in_dim(irrep_rows, cuts_idx * width, width)
    groups = gather_prow(integrals, prow_idx, prow_count)
    block_rows = amplitudes.shape[0] // cuts_count
    others = list(range(1, cuts_count))
    firsts = [jnp.bitwise_xor(cuts_idx, s) * block_rows for s in others] + [cuts_idx * block_rows]
    terms = contract(amplitudes, groups, firsts, block_rows, labels, irrep_cols)
    sent = list(zip(others, terms[:-1]))
    kept = terms[-1]
    half = prow_count // 2
    own_block = prow_idx * cuts_count + cuts_idx
    partner_block = jnp.bitwise_xor(prow_idx, half) * cuts_count + cuts_idx
    mine = lax.dynamic_slice(mirror_row, (own_block * block_rows,), (block_rows,))
    local = mine - partner_block * block_rows
    theirs = lax.dynamic_slice(mirror_row, (partner_block * block_rows,), (block_rows,))
    wanted = theirs - own_block * block_rows
    cols = kept.shape[1]
    pieces = 2 if cols % 16 == 0 else 1
    step = cols // pieces
    results = []
    for j in range(pieces):
        piece = kept[:, j * step:(j + 1) * step]
        for s, part in sent:
            piece = piece + swap(part[:, j * step:(j + 1) * step], "cuts", s)
        if j == pieces - 1 and pieces > 1:
            fetched = swap(jnp.take(piece, wanted, axis=0, mode="clip"), "prow", half)
            results.append(piece - fetched)
        else:
            fetched = swap(piece, "prow", half)
            results.append(piece - jnp.take(fetched, local, axis=0, mode="clip"))
    return jnp.concatenate(results, axis=1) if pieces > 1 else results[0]


def solution(mesh):
    placed = (P("prow", "cuts"), P(("cuts", "prow"), "pcol"), P(), P("pcol"), P())
    return jax.shard_map(
        shards, mesh=mesh, in_specs=placed, out_specs=P(("prow", "cuts"), "pcol"), check_vma=False
    )
```

```python
import jax
import jax.numpy as jnp
from jax import lax
from jax.experimental import pallas as pl
from jax.experimental.pallas import tpu as pltpu
from jax.sharding import PartitionSpec as P


def swap(value, axis, mask):
    return lax.ppermute(value, axis, [(i, i ^ mask) for i in range(lax.axis_size(axis))])


def gather_prow(own, prow_idx, prow_count):
    count = own.shape[0]
    if prow_count == 4 and count % 32 == 0:
        half = count // 2 + count // 16 // 16 * 16
        from_x = swap(own, "prow", 1)
        from_y = swap(own, "prow", 2)
        diag_a = swap(from_y[:half], "prow", 1)
        diag_b = swap(from_x[half:], "prow", 2)
        base = jnp.bitwise_xor(prow_idx, 3) * count
        return [[(own, prow_idx * count)], [(from_y, jnp.bitwise_xor(prow_idx, 2) * count)],
                [(from_x, jnp.bitwise_xor(prow_idx, 1) * count)], [(diag_b, base + half)], [(diag_a, base)]]
    groups = [[(own, prow_idx * count)]]
    for s in range(1, prow_count):
        groups.append([(swap(own, "prow", s), jnp.bitwise_xor(prow_idx, s) * count)])
    return groups


def contract(amplitudes, groups, firsts, rows, labels, irrep_cols):
    bands = [lax.dynamic_slice_in_dim(amplitudes, first, rows, axis=0) for first in firsts]
    terms = [None] * len(bands)
    for g, group in enumerate(groups):
        if g > 0 and (g == len(groups) - 1 or (len(groups) == 5 and g == 3)):
            blocks, held = lax.optimization_barrier((tuple(b for b, _ in group), tuple(terms)))
            group = [(b, o) for b, (_, o) in zip(blocks, group)]
            terms = list(held)
        for i, band in enumerate(bands):
            for b, o in group:
                window = lax.dynamic_slice_in_dim(band, o, b.shape[0], axis=1)
                same = lax.dynamic_slice_in_dim(labels, o, b.shape[0])[:, None] == irrep_cols[None, :]
                blocked = jnp.where(same, b, jnp.zeros_like(b))
                product = jnp.dot(window, blocked, preferred_element_type=jnp.float32)
                terms[i] = product if terms[i] is None else terms[i] + product
    return terms


def shards(amplitudes, integrals, irrep_rows, irrep_cols, mirror_row):
    prow_count = lax.axis_size("prow")
    cuts_count = lax.axis_size("cuts")
    prow_idx = lax.axis_index("prow")
    cuts_idx = lax.axis_index("cuts")
    width = amplitudes.shape[1]
    labels = lax.dynamic_slice_in_dim(irrep_rows, cuts_idx * width, width)
    groups = gather_prow(integrals, prow_idx, prow_count)
    block_rows = amplitudes.shape[0] // cuts_count
    others = list(range(1, cuts_count))
    firsts = [jnp.bitwise_xor(cuts_idx, s) * block_rows for s in others] + [cuts_idx * block_rows]
    terms = contract(amplitudes, groups, firsts, block_rows, labels, irrep_cols)
    sent = list(zip(others, terms[:-1]))
    kept = terms[-1]
    half = prow_count // 2
    own_block = prow_idx * cuts_count + cuts_idx
    partner_block = jnp.bitwise_xor(prow_idx, half) * cuts_count + cuts_idx
    mine = lax.dynamic_slice(mirror_row, (own_block * block_rows,), (block_rows,))
    local = mine - partner_block * block_rows
    theirs = lax.dynamic_slice(mirror_row, (partner_block * block_rows,), (block_rows,))
    wanted = theirs - own_block * block_rows
    cols = kept.shape[1]
    pieces = 2 if cols % 16 == 0 else 1
    step = cols // pieces
    results = []
    for j in range(pieces):
        piece = kept[:, j * step:(j + 1) * step]
        for s, part in sent:
            piece = piece + swap(part[:, j * step:(j + 1) * step], "cuts", s)
        if j == pieces - 1 and pieces > 1:
            fetched = swap(jnp.take(piece, wanted, axis=0, mode="clip"), "prow", half)
            results.append(piece - fetched)
        else:
            fetched = swap(piece, "prow", half)
            results.append(piece - jnp.take(fetched, local, axis=0, mode="clip"))
    return jnp.concatenate(results, axis=1) if pieces > 1 else results[0]


def solution(mesh):
    placed = (P("prow", "cuts"), P(("cuts", "prow"), "pcol"), P(), P("pcol"), P())
    return jax.shard_map(
        shards, mesh=mesh, in_specs=placed, out_specs=P(("prow", "cuts"), "pcol"), check_vma=False
    )
```

```python
import jax
import jax.numpy as jnp
from jax import lax
from jax.experimental import pallas as pl
from jax.experimental.pallas import tpu as pltpu
from jax.sharding import PartitionSpec as P


def swap(value, axis, mask):
    return lax.ppermute(value, axis, [(i, i ^ mask) for i in range(lax.axis_size(axis))])


def gather_prow(own, prow_idx, prow_count):
    count = own.shape[0]
    if prow_count == 4 and count % 32 == 0:
        half = count // 2 + count // 24 // 16 * 16
        from_x = swap(own, "prow", 1)
        from_y = swap(own, "prow", 2)
        diag_a = swap(from_y[:half], "prow", 1)
        diag_b = swap(from_x[half:], "prow", 2)
        base = jnp.bitwise_xor(prow_idx, 3) * count
        return [[(own, prow_idx * count)], [(from_y, jnp.bitwise_xor(prow_idx, 2) * count)],
                [(from_x, jnp.bitwise_xor(prow_idx, 1) * count)], [(diag_a, base), (diag_b, base + half)]]
    groups = [[(own, prow_idx * count)]]
    for s in range(1, prow_count):
        groups.append([(swap(own, "prow", s), jnp.bitwise_xor(prow_idx, s) * count)])
    return groups


def contract(amplitudes, groups, firsts, rows, labels, irrep_cols):
    bands = [lax.dynamic_slice_in_dim(amplitudes, first, rows, axis=0) for first in firsts]
    terms = [None] * len(bands)
    for g, group in enumerate(groups):
        if g == len(groups) - 1 and g > 0:
            blocks, held = lax.optimization_barrier((tuple(b for b, _ in group), tuple(terms)))
            group = [(b, o) for b, (_, o) in zip(blocks, group)]
            terms = list(held)
        for i, band in enumerate(bands):
            for b, o in group:
                window = lax.dynamic_slice_in_dim(band, o, b.shape[0], axis=1)
                same = lax.dynamic_slice_in_dim(labels, o, b.shape[0])[:, None] == irrep_cols[None, :]
                blocked = jnp.where(same, b, jnp.zeros_like(b))
                product = jnp.dot(window, blocked, preferred_element_type=jnp.float32)
                terms[i] = product if terms[i] is None else terms[i] + product
    return terms


def shards(amplitudes, integrals, irrep_rows, irrep_cols, mirror_row):
    prow_count = lax.axis_size("prow")
    cuts_count = lax.axis_size("cuts")
    prow_idx = lax.axis_index("prow")
    cuts_idx = lax.axis_index("cuts")
    width = amplitudes.shape[1]
    labels = lax.dynamic_slice_in_dim(irrep_rows, cuts_idx * width, width)
    groups = gather_prow(integrals, prow_idx, prow_count)
    block_rows = amplitudes.shape[0] // cuts_count
    others = list(range(1, cuts_count))
    firsts = [jnp.bitwise_xor(cuts_idx, s) * block_rows for s in others] + [cuts_idx * block_rows]
    terms = contract(amplitudes, groups, firsts, block_rows, labels, irrep_cols)
    sent = list(zip(others, terms[:-1]))
    kept = terms[-1]
    half = prow_count // 2
    own_block = prow_idx * cuts_count + cuts_idx
    partner_block = jnp.bitwise_xor(prow_idx, half) * cuts_count + cuts_idx
    mine = lax.dynamic_slice(mirror_row, (own_block * block_rows,), (block_rows,))
    local = mine - partner_block * block_rows
    theirs = lax.dynamic_slice(mirror_row, (partner_block * block_rows,), (block_rows,))
    wanted = theirs - own_block * block_rows
    cols = kept.shape[1]
    pieces = 2 if cols % 16 == 0 else 1
    step = cols // pieces
    results = []
    for j in range(pieces):
        piece = kept[:, j * step:(j + 1) * step]
        for s, part in sent:
            piece = piece + swap(part[:, j * step:(j + 1) * step], "cuts", s)
        if j == pieces - 1 and pieces > 1:
            fetched = swap(jnp.take(piece, wanted, axis=0, mode="clip"), "prow", half)
            results.append(piece - fetched)
        else:
            fetched = swap(piece, "prow", half)
            results.append(piece - jnp.take(fetched, local, axis=0, mode="clip"))
    return jnp.concatenate(results, axis=1) if pieces > 1 else results[0]


def solution(mesh):
    placed = (P("prow", "cuts"), P(("cuts", "prow"), "pcol"), P(), P("pcol"), P())
    return jax.shard_map(
        shards, mesh=mesh, in_specs=placed, out_specs=P(("prow", "cuts"), "pcol"), check_vma=False
    )
```
